32 devices in a mesh: region: 4 (over y, x), col: 8 (over z, core).
Axes of the slice: x: 2, y: 2, z: 4, core: 2. Of those that a mesh axis runs over, the one named last changes fastest.
Arguments:
- tiles: float32 [1536, 128, 128], P(('region', 'col')), may hold values from -0.109375 to 0.109375
- tile_rows: int32 [1536], P(('region', 'col')), may hold values from 0 to 1
- tile_cols: int32 [1536], P(('region', 'col')), may hold values from 0 to 15
- tile_count: int32 [32], P(('region', 'col')), may hold values from 12 to 48, as said below
- rhs: float32 [64, 128], P(('region', 'col')), may hold values from -6 to 6
- base_cost: float32 [64, 128], P(('region', 'col')), may hold values from 0.1 to 1
- upper: float32 [64, 128], P(('region', 'col')), may hold values from 0.5 to 4
- primal: float32 [64, 16, 128], P(('region', 'col')), may hold values from 0 to 1
- dual: float32 [64, 16, 128], P(('region', 'col')), may hold values from 0 to 1
- price_levels: float32 [32, 128], replicated, may hold values from 0.5 to 2
- scenario_ids: int32 [16], replicated, may hold values from 0 to 31
Outputs:
- primal_out: float32 [64, 16, 128], P(('region', 'col'))
- dual_out: float32 [64, 16, 128], P(('region', 'col'))
- weight_out: float32 [16], replicated
The draws below stay inside these ranges and needn't reach their ends.
Inputs may be any that keep to these rules, and one draw needn't show every extreme that they name: `tile_count`: slots at or past a device's count are padding and hold no part of the matrix; in every draw some device has all 48 slots live.
All inputs are finite; a program needn't handle non-finite values.
Results may differ from the reference program's by a relative error of at most 0.0001.
Values sent between devices are 32-bit elements; how exact they have to be, the bound alone decides.
No kernel may reach another device: no remote copies, remote signals or barrier semaphores. Data moves between devices by JAX's collectives and lax.ppermute only.
A program may use at most 64 MiB of HBM per device.

```python
import math
import jax
import jax.numpy as jnp
from jax import lax

TILE = 128
SCEN = 16
NPRICE = 32
ITERS = 2
TPR = 24
RB_DEV = 2
TILES_DEV = 48
CB_REG = 16
CB_ALL = 64
RB_ALL = 64
TILE_SLOTS = 1536
N_COL = 8


def draw_tile_count(key, part):
    devices = TILE_SLOTS // TILES_DEV
    least = max(1, TILES_DEV // 4)
    counts = jax.random.randint(jax.random.fold_in(key, 11), (devices,), least, TILES_DEV + 1)
    full = jax.random.randint(jax.random.fold_in(key, 12), (), 0, devices)
    return counts.at[full].set(TILES_DEV).astype(jnp.int32)


def place_ends(entries, own_key, low, high):
    spot = [jax.random.randint(jax.random.fold_in(own_key, axis), (), 0, length) for axis, length in enumerate(entries.shape)]
    longest = entries.shape.index(max(entries.shape))
    neighbour = spot[:longest] + [(spot[longest] + 1) % entries.shape[longest]] + spot[longest + 1:]
    return entries.at[tuple(spot)].set(low).at[tuple(neighbour)].set(high)


def levels(own_key, shape, split, low, largest):
    gain, own = 1.0, jax.random.fold_in(own_key, 6)
    for position, parts in split:
        steps = jnp.exp(jax.random.uniform(jax.random.fold_in(own, position), (parts,), jnp.float32, low / len(split), largest / len(split)))
        gain = gain * jnp.repeat(steps, shape[position] // parts).reshape([-1 if axis == position else 1 for axis in range(len(shape))])
    return gain


def noise(rng, shape, deviation, reach, cuts=(), kind=jnp.bfloat16):
    factor_of = levels(rng, shape, cuts, -0.22, 0.18) if cuts else 1.0
    result = jax.random.normal(rng, shape, jnp.float32) * deviation * factor_of
    return jnp.minimum(jnp.maximum(result, -reach), reach).astype(kind)


def setup_inputs(seed: int = 0) -> dict:
    splits = jax.random.split(jax.random.key(seed), 12)
    return {
        "tiles": noise(splits[0], (TILE_SLOTS, TILE, TILE), (TPR * TILE) ** -0.5, 0.109375, ((0, 32),), jnp.float32),
        "tile_rows": place_ends(jax.random.randint(splits[1], (TILE_SLOTS,), 0, RB_DEV), jax.random.fold_in(splits[1], 1), 0, RB_DEV - 1).astype(jnp.int32),
        "tile_cols": place_ends(jax.random.randint(splits[2], (TILE_SLOTS,), 0, CB_REG), jax.random.fold_in(splits[2], 1), 0, CB_REG - 1).astype(jnp.int32),
        "tile_count": draw_tile_count(jax.random.fold_in(splits[11], 71), 0),
        "rhs": noise(splits[4], (RB_ALL, TILE), 1.0, 6.0, ((0, 32),), jnp.float32),
        "base_cost": jnp.clip(jnp.exp(math.log(1.0) - 2.3025851 * jax.random.uniform(splits[5], (CB_ALL, TILE), jnp.float32) ** levels(splits[5], (CB_ALL, TILE), ((0, 32),), -0.2, 0.2)), 0.1, 1.0),
        "upper": jnp.clip(jnp.exp(math.log(4.0) - 2.0794415 * jax.random.uniform(splits[6], (CB_ALL, TILE), jnp.float32) ** levels(splits[6], (CB_ALL, TILE), ((0, 32),), -0.2, 0.2)), 0.5, 4.0),
        "primal": jnp.clip(1.0 * jax.random.uniform(splits[7], (CB_ALL, SCEN, TILE), jnp.float32) ** levels(splits[7], (CB_ALL, SCEN, TILE), ((0, 32),), -0.2, 0.2), 0.0, 1.0),
        "dual": jnp.clip(1.0 * jax.random.uniform(splits[8], (RB_ALL, SCEN, TILE), jnp.float32) ** levels(splits[8], (RB_ALL, SCEN, TILE), ((0, 32),), -0.2, 0.2), 0.0, 1.0),
        "price_levels": jnp.clip(jnp.exp(jax.random.uniform(splits[9], (NPRICE, TILE), jnp.float32, math.log(0.5), math.log(2.0))), 0.5, 2.0),
        "scenario_ids": place_ends(jax.random.randint(splits[10], (SCEN,), 0, NPRICE), jax.random.fold_in(splits[10], 1), 0, NPRICE - 1).astype(jnp.int32),
    }


def reference(tiles, tile_rows, tile_cols, tile_count, rhs, base_cost, upper, primal, dual, price_levels, scenario_ids):
    hp = lax.Precision.HIGHEST
    slot = jnp.arange(TILE_SLOTS, dtype=jnp.int32)
    device = slot // TILES_DEV
    local = slot % TILES_DEV
    live = (local < tile_count[device]).astype(jnp.float32)
    grow = (device * RB_DEV + tile_rows).astype(jnp.int32)
    gcol = (device // N_COL * CB_REG + tile_cols).astype(jnp.int32)
    choose = (scenario_ids[:, None] == jnp.arange(NPRICE, dtype=jnp.int32)[None, :]).astype(jnp.float32)
    factor = jnp.dot(choose, price_levels, precision=hp)
    cost = base_cost[:, None, :] * factor[None, :, :]
    sq_a = jnp.sum(lax.optimization_barrier(jnp.sum(tiles * tiles, axis=(1, 2))) * live)
    sq_c = lax.optimization_barrier(jnp.sum(cost * cost, axis=(0, 2)))
    sq_b = jnp.sum(rhs * rhs)
    eta = 0.5 / jnp.sqrt(sq_a / (TILE * RB_ALL))
    weight = jnp.sqrt(sq_c) / jnp.sqrt(sq_b)
    for step in range(ITERS):
        tau = (eta / weight)[None, :, None]
        sigma = (eta * weight)[None, :, None]
        contrib = jnp.einsum('tij,tsi->tsj', tiles, dual[grow], precision=hp) * live[:, None, None]
        grad = jax.ops.segment_sum(contrib, gcol, num_segments=CB_ALL)
        new_primal = jnp.clip(primal - tau * (cost - grad), 0.0, upper[:, None, :])
        point = 2.0 * new_primal - primal
        image = jnp.einsum('tij,tsj->tsi', tiles, point[gcol], precision=hp) * live[:, None, None]
        product = jax.ops.segment_sum(image, grow, num_segments=RB_ALL)
        new_dual = jnp.maximum(dual + sigma * (rhs[:, None, :] - product), 0.0)
        step_x = lax.optimization_barrier(jnp.sum((new_primal - primal) ** 2, axis=(0, 2)))
        step_y = lax.optimization_barrier(jnp.sum((new_dual - dual) ** 2, axis=(0, 2)))
        weight = jnp.sqrt(weight * jnp.sqrt((step_x + 1e-06) / (step_y + 1e-06)))
        primal, dual = (new_primal, new_dual)
    return (primal, dual, weight)
```

```python
import jax
import jax.numpy as jnp
from jax import lax
from jax.sharding import PartitionSpec as P

ITERS = 2


def _pow2(n):
    return n >= 1 and (n & (n - 1)) == 0


def _exchange(x, axis, n, bit):
    return lax.ppermute(x, axis, [(i, i ^ (1 << bit)) for i in range(n)])


def _rounds(axis, sums, chunk=None):
    n = lax.axis_size(axis)
    if not _pow2(n):
        sums = [lax.psum(s, axis) for s in sums]
        if chunk is not None:
            chunk = lax.all_gather(chunk, axis, axis=0, tiled=False)
        return sums, chunk
    shapes = [s.shape for s in sums]
    sizes = [s.size for s in sums]
    me = lax.axis_index(axis)
    if chunk is not None:
        chunk = chunk[None]
    bits = n.bit_length() - 1
    for bit in range(bits):
        parts = [s.reshape(-1) for s in sums]
        if chunk is not None:
            parts.append(chunk.reshape(-1))
        flat = jnp.concatenate(parts) if len(parts) > 1 else parts[0]
        got = _exchange(flat, axis, n, bit)
        off = 0
        new_sums = []
        for shape, size, s in zip(shapes, sizes, sums):
            new_sums.append(s + got[off : off + size].reshape(shape))
            off += size
        sums = new_sums
        if chunk is not None:
            theirs = got[off:].reshape(chunk.shape)
            low = ((me >> bit) & 1) == 0
            chunk = jnp.where(
                low,
                jnp.concatenate([chunk, theirs], axis=0),
                jnp.concatenate([theirs, chunk], axis=0),
            )
    return sums, chunk


def local(
    tiles,
    tile_rows,
    tile_cols,
    tile_count,
    rhs,
    base_cost,
    upper,
    primal,
    dual,
    price_levels,
    scenario_ids,
):
    hp = lax.Precision.HIGHEST
    ntiles = tiles.shape[0]
    row_blocks = rhs.shape[0]
    own_blocks = base_cost.shape[0]
    scenarios = primal.shape[1]
    lanes = primal.shape[2]
    ncol = lax.axis_size("col")
    region_blocks = own_blocks * ncol
    devices = lax.axis_size(("region", "col"))
    me = lax.axis_index("col")
    live = (jnp.arange(ntiles, dtype=jnp.int32) < tile_count[0]).astype(jnp.float32)
    row_select = (tile_rows[:, None] == jnp.arange(row_blocks, dtype=jnp.int32)[None, :]).astype(
        jnp.float32
    )
    row_live = row_select * live[:, None]
    col_select = (tile_cols[:, None] == jnp.arange(region_blocks, dtype=jnp.int32)[None, :]).astype(
        jnp.float32
    )
    col_live = col_select * live[:, None]
    choose = (
        scenario_ids[:, None] == jnp.arange(price_levels.shape[0], dtype=jnp.int32)[None, :]
    ).astype(jnp.float32)
    factor = jnp.dot(choose, price_levels, precision=hp)
    cost = base_cost[:, None, :] * factor[None, :, :]
    local_a = jnp.sum(jnp.sum(tiles * tiles, axis=(1, 2)) * live)
    local_c = jnp.sum(cost * cost, axis=(0, 2))
    local_b = jnp.sum(rhs * rhs)
    width = scenarios * lanes

    def transposed_product(dual):
        dual_rows = jnp.dot(row_select, dual.reshape(row_blocks, width), precision=hp).reshape(
            ntiles, scenarios, lanes
        )
        contrib = jnp.einsum("tij,tsi->tsj", tiles, dual_rows, precision=hp)
        return jnp.dot(col_live.T, contrib.reshape(ntiles, width), precision=hp).reshape(
            region_blocks, scenarios, lanes
        )

    (local_a, local_c, local_b), _ = _rounds(
        "region", [local_a.reshape(1), local_c, local_b.reshape(1)]
    )
    own = jnp.concatenate([primal, base_cost[:, None, :], upper[:, None, :]], axis=1)
    partial_value = transposed_product(dual)
    (grad, sq_a, sq_c, sq_b), gathered = _rounds(
        "col", [partial_value, local_a, local_c, local_b], own
    )
    gathered = gathered.reshape(region_blocks, scenarios + 2, lanes)
    primal_reg = gathered[:, :scenarios, :]
    cost_reg = gathered[:, scenarios, :][:, None, :] * factor[None, :, :]
    upper_reg = gathered[:, scenarios + 1, :][:, None, :]
    eta = 0.5 / jnp.sqrt(sq_a[0] / (lanes * row_blocks * devices))
    weight = jnp.sqrt(sq_c) / jnp.sqrt(sq_b[0])
    for step in range(ITERS):
        if step > 0:
            (step_x, part_y), _ = _rounds("region", [local_x, local_y])
            partial_value = transposed_product(dual)
            (grad, step_y), _ = _rounds("col", [partial_value, part_y])
            weight = jnp.sqrt(weight * jnp.sqrt((step_x + 1e-06) / (step_y + 1e-06)))
        tau = (eta / weight)[None, :, None]
        sigma = (eta * weight)[None, :, None]
        new_primal = jnp.clip(primal_reg - tau * (cost_reg - grad), 0.0, upper_reg)
        point = 2.0 * new_primal - primal_reg
        selected = jnp.dot(col_select, point.reshape(region_blocks, width), precision=hp).reshape(
            ntiles, scenarios, lanes
        )
        image = jnp.einsum("tij,tsj->tsi", tiles, selected, precision=hp)
        product = jnp.dot(row_live.T, image.reshape(ntiles, width), precision=hp).reshape(
            row_blocks, scenarios, lanes
        )
        new_dual = jnp.maximum(dual + sigma * (rhs[:, None, :] - product), 0.0)
        local_x = jnp.sum((new_primal - primal_reg) ** 2, axis=(0, 2))
        local_y = jnp.sum((new_dual - dual) ** 2, axis=(0, 2))
        primal_reg, dual = (new_primal, new_dual)
    (step_x, part_y), _ = _rounds("region", [local_x, local_y])
    (step_y,), _ = _rounds("col", [part_y])
    weight = jnp.sqrt(weight * jnp.sqrt((step_x + 1e-06) / (step_y + 1e-06)))
    primal_out = lax.dynamic_slice_in_dim(primal_reg, me * own_blocks, own_blocks, axis=0)
    return (primal_out, dual, weight)


def solution(mesh):
    placed = (
        P(("region", "col"), None, None),
        P(("region", "col")),
        P(("region", "col")),
        P(("region", "col")),
        P(("region", "col"), None),
        P(("region", "col"), None),
        P(("region", "col"), None),
        P(("region", "col"), None, None),
        P(("region", "col"), None, None),
        P(),
        P(),
    )
    return jax.shard_map(
        local,
        mesh=mesh,
        in_specs=placed,
        out_specs=(P(("region", "col"), None, None), P(("region", "col"), None, None), P()),
        check_vma=False,
    )
```

```python
import jax
import jax.numpy as jnp
from jax import lax
from jax.sharding import PartitionSpec as P

ITERS = 2


def _pow2(n):
    return n >= 1 and (n & (n - 1)) == 0


def _exchange(x, axis, n, bit):
    return lax.ppermute(x, axis, [(i, i ^ (1 << bit)) for i in range(n)])


def _rounds(axis, total, own=None):
    n = lax.axis_size(axis)
    if not _pow2(n):
        total = lax.psum(total, axis)
        if own is not None:
            own = lax.all_gather(own, axis, axis=0, tiled=True)
        return total, own
    me = lax.axis_index(axis)
    rows = total.shape[0]
    buf = None
    if own is not None:
        g = own.shape[0]
        buf = jnp.zeros((n * g, own.shape[1]), own.dtype)
        buf = lax.dynamic_update_slice_in_dim(buf, own, me * g, axis=0)
    for bit in range(n.bit_length() - 1):
        if buf is None:
            got = _exchange(total, axis, n, bit)
            total = total + got
            continue
        span = (1 << bit) * g
        mine = lax.dynamic_slice_in_dim(buf, ((me >> bit) << bit) * g, span, axis=0)
        got = _exchange(jnp.concatenate([total, mine], axis=0), axis, n, bit)
        total = total + got[:rows]
        theirs = ((me ^ (1 << bit)) >> bit) << bit
        buf = lax.dynamic_update_slice_in_dim(buf, got[rows:], theirs * g, axis=0)
    return total, buf


def _pack(lanes, *vectors):
    small = jnp.zeros((8, lanes), jnp.float32)
    for row, v in enumerate(vectors):
        v = jnp.reshape(v, (-1,))
        small = small.at[row, : v.shape[0]].set(v)
    return small


def local(
    tiles,
    tile_rows,
    tile_cols,
    tile_count,
    rhs,
    base_cost,
    upper,
    primal,
    dual,
    price_levels,
    scenario_ids,
):
    hp = lax.Precision.HIGHEST
    ntiles = tiles.shape[0]
    row_blocks = rhs.shape[0]
    own_blocks = base_cost.shape[0]
    scenarios = primal.shape[1]
    lanes = primal.shape[2]
    ncol = lax.axis_size("col")
    region_blocks = own_blocks * ncol
    devices = lax.axis_size(("region", "col"))
    me = lax.axis_index("col")
    live = (jnp.arange(ntiles, dtype=jnp.int32) < tile_count[0]).astype(jnp.float32)
    row_select = (tile_rows[:, None] == jnp.arange(row_blocks, dtype=jnp.int32)[None, :]).astype(
        jnp.float32
    )
    row_live = row_select * live[:, None]
    col_select = (tile_cols[:, None] == jnp.arange(region_blocks, dtype=jnp.int32)[None, :]).astype(
        jnp.float32
    )
    col_live = col_select * live[:, None]
    choose = (
        scenario_ids[:, None] == jnp.arange(price_levels.shape[0], dtype=jnp.int32)[None, :]
    ).astype(jnp.float32)
    factor = jnp.dot(choose, price_levels, precision=hp)
    cost = base_cost[:, None, :] * factor[None, :, :]
    local_a = jnp.sum(jnp.sum(tiles * tiles, axis=(1, 2)) * live)
    local_c = jnp.sum(cost * cost, axis=(0, 2))
    local_b = jnp.sum(rhs * rhs)
    width = scenarios * lanes

    def transposed_product(dual):
        dual_rows = jnp.dot(row_select, dual.reshape(row_blocks, width), precision=hp).reshape(
            ntiles, scenarios, lanes
        )
        contrib = jnp.einsum("tij,tsi->tsj", tiles, dual_rows, precision=hp)
        return jnp.dot(col_live.T, contrib.reshape(ntiles, width), precision=hp).reshape(
            region_blocks, scenarios, lanes
        )

    small, _ = _rounds("region", _pack(lanes, local_c, local_a, local_b))
    own_rows = own_blocks * (scenarios + 2)
    pad = -own_rows % 8
    own = jnp.concatenate(
        [
            primal.reshape(own_blocks * scenarios, lanes),
            base_cost,
            upper,
            jnp.zeros((pad, lanes), jnp.float32),
        ],
        axis=0,
    )
    grad_rows = region_blocks * scenarios
    partial_value = transposed_product(dual).reshape(grad_rows, lanes)
    summed, gathered = _rounds("col", jnp.concatenate([partial_value, small], axis=0), own)
    grad = summed[:grad_rows].reshape(region_blocks, scenarios, lanes)
    sq_c = summed[grad_rows, :scenarios]
    sq_a = summed[grad_rows + 1, 0]
    sq_b = summed[grad_rows + 2, 0]
    gathered = gathered.reshape(ncol, own_rows + pad, lanes)
    primal_reg = gathered[:, : own_blocks * scenarios].reshape(region_blocks, scenarios, lanes)
    base_reg = gathered[:, own_blocks * scenarios : own_blocks * (scenarios + 1)].reshape(
        region_blocks, lanes
    )
    upper_reg = gathered[:, own_blocks * (scenarios + 1) : own_rows].reshape(region_blocks, lanes)
    cost_reg = base_reg[:, None, :] * factor[None, :, :]
    upper_reg = upper_reg[:, None, :]
    eta = 0.5 / jnp.sqrt(sq_a / (lanes * row_blocks * devices))
    weight = jnp.sqrt(sq_c) / jnp.sqrt(sq_b)
    for step in range(ITERS):
        if step > 0:
            steps, _ = _rounds("region", _pack(lanes, local_x, local_y))
            partial_value = transposed_product(dual).reshape(grad_rows, lanes)
            summed, _ = _rounds(
                "col", jnp.concatenate([partial_value, _pack(lanes, steps[1, :scenarios])], axis=0)
            )
            grad = summed[:grad_rows].reshape(region_blocks, scenarios, lanes)
            step_x = steps[0, :scenarios]
            step_y = summed[grad_rows, :scenarios]
            weight = jnp.sqrt(weight * jnp.sqrt((step_x + 1e-06) / (step_y + 1e-06)))
        tau = (eta / weight)[None, :, None]
        sigma = (eta * weight)[None, :, None]
        new_primal = jnp.clip(primal_reg - tau * (cost_reg - grad), 0.0, upper_reg)
        point = 2.0 * new_primal - primal_reg
        selected = jnp.dot(col_select, point.reshape(region_blocks, width), precision=hp).reshape(
            ntiles, scenarios, lanes
        )
        image = jnp.einsum("tij,tsj->tsi", tiles, selected, precision=hp)
        product = jnp.dot(row_live.T, image.reshape(ntiles, width), precision=hp).reshape(
            row_blocks, scenarios, lanes
        )
        new_dual = jnp.maximum(dual + sigma * (rhs[:, None, :] - product), 0.0)
        local_x = jnp.sum((new_primal - primal_reg) ** 2, axis=(0, 2))
        local_y = jnp.sum((new_dual - dual) ** 2, axis=(0, 2))
        primal_reg, dual = (new_primal, new_dual)
    steps, _ = _rounds("region", _pack(lanes, local_x, local_y))
    summed, _ = _rounds("col", _pack(lanes, steps[1, :scenarios]))
    step_x = steps[0, :scenarios]
    step_y = summed[0, :scenarios]
    weight = jnp.sqrt(weight * jnp.sqrt((step_x + 1e-06) / (step_y + 1e-06)))
    primal_out = lax.dynamic_slice_in_dim(primal_reg, me * own_blocks, own_blocks, axis=0)
    return (primal_out, dual, weight)


def solution(mesh):
    placed = (
        P(("region", "col"), None, None),
        P(("region", "col")),
        P(("region", "col")),
        P(("region", "col")),
        P(("region", "col"), None),
        P(("region", "col"), None),
        P(("region", "col"), None),
        P(("region", "col"), None, None),
        P(("region", "col"), None, None),
        P(),
        P(),
    )
    return jax.shard_map(
        local,
        mesh=mesh,
        in_specs=placed,
        out_specs=(P(("region", "col"), None, None), P(("region", "col"), None, None), P()),
        check_vma=False,
    )
```

```python
import jax
import jax.numpy as jnp
from jax import lax
from jax.sharding import PartitionSpec as P

ITERS = 2


def _pow2(n):
    return n >= 1 and (n & (n - 1)) == 0


def _exchange(x, axis, n, bit):
    return lax.ppermute(x, axis, [(i, i ^ (1 << bit)) for i in range(n)])


def _rounds(axis, total, owns=()):
    n = lax.axis_size(axis)
    if not _pow2(n):
        total = lax.psum(total, axis)
        owns = [lax.all_gather(o, axis, axis=0, tiled=True) for o in owns]
        return total, owns
    me = lax.axis_index(axis)
    rows = total.shape[0]
    bufs = []
    for o in owns:
        buf = jnp.zeros((n * o.shape[0],) + o.shape[1:], o.dtype)
        bufs.append(lax.dynamic_update_slice_in_dim(buf, o, me * o.shape[0], axis=0))
    for bit in range(n.bit_length() - 1):
        if not bufs:
            total = total + _exchange(total, axis, n, bit)
            continue
        start = (me >> bit) << bit
        theirs = ((me ^ (1 << bit)) >> bit) << bit
        parts = [total]
        for o, buf in zip(owns, bufs):
            g = o.shape[0]
            parts.append(lax.dynamic_slice_in_dim(buf, start * g, (1 << bit) * g, axis=0))
        got = _exchange(jnp.concatenate(parts, axis=0), axis, n, bit)
        total = total + got[:rows]
        off = rows
        for i, o in enumerate(owns):
            span = (1 << bit) * o.shape[0]
            bufs[i] = lax.dynamic_update_slice_in_dim(
                bufs[i], got[off : off + span], theirs * o.shape[0], axis=0
            )
            off += span
    return total, bufs


def _pack(lanes, *vectors):
    flat = jnp.concatenate([jnp.reshape(v, (-1,)) for v in vectors])
    size = 8 * lanes
    flat = jnp.concatenate([flat, jnp.zeros((size - flat.shape[0],), flat.dtype)])
    return flat.reshape(8, lanes)


def _unpack(small, *sizes):
    flat = small.reshape(-1)
    out, off = [], 0
    for s in sizes:
        out.append(flat[off : off + s])
        off += s
    return out


def local(
    tiles,
    tile_rows,
    tile_cols,
    tile_count,
    rhs,
    base_cost,
    upper,
    primal,
    dual,
    price_levels,
    scenario_ids,
):
    hp = lax.Precision.HIGHEST
    ntiles = tiles.shape[0]
    row_blocks = rhs.shape[0]
    own_blocks = base_cost.shape[0]
    scenarios = primal.shape[1]
    lanes = primal.shape[2]
    ncol = lax.axis_size("col")
    region_blocks = own_blocks * ncol
    devices = lax.axis_size(("region", "col"))
    me = lax.axis_index("col")
    live = (jnp.arange(ntiles, dtype=jnp.int32) < tile_count[0]).astype(jnp.float32)
    row_select = (tile_rows[:, None] == jnp.arange(row_blocks, dtype=jnp.int32)[None, :]).astype(
        jnp.float32
    )
    row_live = row_select * live[:, None]
    col_select = (tile_cols[:, None] == jnp.arange(region_blocks, dtype=jnp.int32)[None, :]).astype(
        jnp.float32
    )
    col_live = col_select * live[:, None]
    choose = (
        scenario_ids[:, None] == jnp.arange(price_levels.shape[0], dtype=jnp.int32)[None, :]
    ).astype(jnp.float32)
    factor = jnp.dot(choose, price_levels, precision=hp)
    cost = base_cost[:, None, :] * factor[None, :, :]
    local_a = jnp.sum(jnp.sum(tiles * tiles, axis=(1, 2)) * live)
    local_c = jnp.sum(cost * cost, axis=(0, 2))
    local_b = jnp.sum(rhs * rhs)
    width = scenarios * lanes

    def transposed_product(dual):
        dual_rows = jnp.dot(row_select, dual.reshape(row_blocks, width), precision=hp).reshape(
            ntiles, scenarios, lanes
        )
        contrib = jnp.einsum("tij,tsi->tsj", tiles, dual_rows, precision=hp)
        return jnp.dot(col_live.T, contrib.reshape(ntiles, width), precision=hp).reshape(
            region_blocks, scenarios, lanes
        )

    norms = jnp.concatenate([local_a.reshape(1), local_c, local_b.reshape(1)])
    norms, _ = _rounds("region", norms)
    own_misc = jnp.concatenate(
        [base_cost, upper, jnp.zeros((-2 * own_blocks % 8, lanes), jnp.float32)], axis=0
    )
    misc_rows = own_misc.shape[0]
    grad_rows = region_blocks * scenarios
    partial_value = transposed_product(dual).reshape(grad_rows, lanes)
    summed, (primal_reg, misc) = _rounds(
        "col",
        jnp.concatenate([partial_value, _pack(lanes, norms)], axis=0),
        (primal.reshape(own_blocks * scenarios, lanes), own_misc),
    )
    grad = summed[:grad_rows].reshape(region_blocks, scenarios, lanes)
    (norms,) = _unpack(summed[grad_rows:], scenarios + 2)
    sq_a, sq_c, sq_b = norms[0], norms[1 : scenarios + 1], norms[scenarios + 1]
    primal_reg = primal_reg.reshape(region_blocks, scenarios, lanes)
    misc = misc.reshape(ncol, misc_rows, lanes)
    base_reg = misc[:, :own_blocks].reshape(region_blocks, lanes)
    upper_reg = misc[:, own_blocks : 2 * own_blocks].reshape(region_blocks, lanes)
    cost_reg = base_reg[:, None, :] * factor[None, :, :]
    upper_reg = upper_reg[:, None, :]
    eta = 0.5 / jnp.sqrt(sq_a / (lanes * row_blocks * devices))
    weight = jnp.sqrt(sq_c) / jnp.sqrt(sq_b)
    for step in range(ITERS):
        if step > 0:
            steps, _ = _rounds("region", jnp.concatenate([local_x, local_y]))
            partial_value = transposed_product(dual).reshape(grad_rows, lanes)
            summed, _ = _rounds(
                "col", jnp.concatenate([partial_value, _pack(lanes, steps[scenarios:])], axis=0)
            )
            grad = summed[:grad_rows].reshape(region_blocks, scenarios, lanes)
            step_x = steps[:scenarios]
            (step_y,) = _unpack(summed[grad_rows:], scenarios)
            weight = jnp.sqrt(weight * jnp.sqrt((step_x + 1e-06) / (step_y + 1e-06)))
        tau = (eta / weight)[None, :, None]
        sigma = (eta * weight)[None, :, None]
        new_primal = jnp.clip(primal_reg - tau * (cost_reg - grad), 0.0, upper_reg)
        point = 2.0 * new_primal - primal_reg
        selected = jnp.dot(col_select, point.reshape(region_blocks, width), precision=hp).reshape(
            ntiles, scenarios, lanes
        )
        image = jnp.einsum("tij,tsj->tsi", tiles, selected, precision=hp)
        product = jnp.dot(row_live.T, image.reshape(ntiles, width), precision=hp).reshape(
            row_blocks, scenarios, lanes
        )
        new_dual = jnp.maximum(dual + sigma * (rhs[:, None, :] - product), 0.0)
        local_x = jnp.sum((new_primal - primal_reg) ** 2, axis=(0, 2))
        local_y = jnp.sum((new_dual - dual) ** 2, axis=(0, 2))
        primal_reg, dual = (new_primal, new_dual)
    steps, _ = _rounds("region", jnp.concatenate([local_x, local_y]))
    step_y, _ = _rounds("col", steps[scenarios:])
    step_x = steps[:scenarios]
    weight = jnp.sqrt(weight * jnp.sqrt((step_x + 1e-06) / (step_y + 1e-06)))
    primal_out = lax.dynamic_slice_in_dim(primal_reg, me * own_blocks, own_blocks, axis=0)
    return (primal_out, dual, weight)


def solution(mesh):
    placed = (
        P(("region", "col"), None, None),
        P(("region", "col")),
        P(("region", "col")),
        P(("region", "col")),
        P(("region", "col"), None),
        P(("region", "col"), None),
        P(("region", "col"), None),
        P(("region", "col"), None, None),
        P(("region", "col"), None, None),
        P(),
        P(),
    )
    return jax.shard_map(
        local,
        mesh=mesh,
        in_specs=placed,
        out_specs=(P(("region", "col"), None, None), P(("region", "col"), None, None), P()),
        check_vma=False,
    )
```

```python
import jax
import jax.numpy as jnp
from jax import lax
from jax.sharding import PartitionSpec as P

ITERS = 2


def _pow2(n):
    return n >= 1 and (n & (n - 1)) == 0


def _exchange(x, axis, n, bit):
    return lax.ppermute(x, axis, [(i, i ^ (1 << bit)) for i in range(n)])


def _rounds(axis, sums, own=None):
    n = lax.axis_size(axis)
    if not _pow2(n):
        sums = [lax.psum(s, axis) for s in sums]
        if own is not None:
            own = lax.all_gather(own, axis, axis=0, tiled=False)
        return sums, own
    shapes = [s.shape for s in sums]
    sizes = [s.size for s in sums]
    me = lax.axis_index(axis)
    buf = None
    if own is not None:
        buf = jnp.zeros((n,) + own.shape, own.dtype)
        buf = lax.dynamic_update_index_in_dim(buf, own, me, 0)
    for bit in range(n.bit_length() - 1):
        parts = [s.reshape(-1) for s in sums]
        if buf is not None:
            used = sum(sizes)
            parts.append(jnp.zeros((-used % 1024,), jnp.float32))
            start = (me >> bit) << bit
            parts.append(lax.dynamic_slice_in_dim(buf, start, 1 << bit, axis=0).reshape(-1))
        flat = jnp.concatenate(parts) if len(parts) > 1 else parts[0]
        got = _exchange(flat, axis, n, bit)
        off = 0
        new_sums = []
        for shape, size, s in zip(shapes, sizes, sums):
            new_sums.append(s + got[off : off + size].reshape(shape))
            off += size
        sums = new_sums
        if buf is not None:
            off += -off % 1024
            theirs = ((me ^ (1 << bit)) >> bit) << bit
            chunk = got[off:].reshape((1 << bit,) + own.shape)
            buf = lax.dynamic_update_slice_in_dim(buf, chunk, theirs, axis=0)
    return sums, buf


def local(
    tiles,
    tile_rows,
    tile_cols,
    tile_count,
    rhs,
    base_cost,
    upper,
    primal,
    dual,
    price_levels,
    scenario_ids,
):
    hp = lax.Precision.HIGHEST
    ntiles = tiles.shape[0]
    row_blocks = rhs.shape[0]
    own_blocks = base_cost.shape[0]
    scenarios = primal.shape[1]
    lanes = primal.shape[2]
    ncol = lax.axis_size("col")
    region_blocks = own_blocks * ncol
    devices = lax.axis_size(("region", "col"))
    me = lax.axis_index("col")
    live = (jnp.arange(ntiles, dtype=jnp.int32) < tile_count[0]).astype(jnp.float32)
    row_select = (tile_rows[:, None] == jnp.arange(row_blocks, dtype=jnp.int32)[None, :]).astype(
        jnp.float32
    )
    row_live = row_select * live[:, None]
    col_select = (tile_cols[:, None] == jnp.arange(region_blocks, dtype=jnp.int32)[None, :]).astype(
        jnp.float32
    )
    col_live = col_select * live[:, None]
    choose = (
        scenario_ids[:, None] == jnp.arange(price_levels.shape[0], dtype=jnp.int32)[None, :]
    ).astype(jnp.float32)
    factor = jnp.dot(choose, price_levels, precision=hp)
    cost = base_cost[:, None, :] * factor[None, :, :]
    local_a = jnp.sum(jnp.sum(tiles * tiles, axis=(1, 2)) * live)
    local_c = jnp.sum(cost * cost, axis=(0, 2))
    local_b = jnp.sum(rhs * rhs)
    width = scenarios * lanes

    def transposed_product(dual):
        dual_rows = jnp.dot(row_select, dual.reshape(row_blocks, width), precision=hp).reshape(
            ntiles, scenarios, lanes
        )
        contrib = jnp.einsum("tij,tsi->tsj", tiles, dual_rows, precision=hp)
        return jnp.dot(col_live.T, contrib.reshape(ntiles, width), precision=hp).reshape(
            region_blocks, scenarios, lanes
        )

    (local_a, local_c, local_b), _ = _rounds(
        "region", [local_a.reshape(1), local_c, local_b.reshape(1)]
    )
    own_rows = own_blocks * (scenarios + 2)
    own = jnp.concatenate(
        [
            primal.reshape(own_blocks * scenarios, lanes),
            base_cost,
            upper,
            jnp.zeros((-own_rows % 8, lanes), jnp.float32),
        ],
        axis=0,
    )
    partial_value = transposed_product(dual)
    (grad, sq_a, sq_c, sq_b), gathered = _rounds(
        "col", [partial_value, local_a, local_c, local_b], own
    )
    primal_reg = gathered[:, : own_blocks * scenarios].reshape(region_blocks, scenarios, lanes)
    base_reg = gathered[:, own_blocks * scenarios : own_blocks * (scenarios + 1)]
    upper_reg = gathered[:, own_blocks * (scenarios + 1) : own_rows]
    cost_reg = base_reg.reshape(region_blocks, lanes)[:, None, :] * factor[None, :, :]
    upper_reg = upper_reg.reshape(region_blocks, lanes)[:, None, :]
    eta = 0.5 / jnp.sqrt(sq_a[0] / (lanes * row_blocks * devices))
    weight = jnp.sqrt(sq_c) / jnp.sqrt(sq_b[0])
    for step in range(ITERS):
        if step > 0:
            (step_x, part_y), _ = _rounds("region", [local_x, local_y])
            partial_value = transposed_product(dual)
            (grad, step_y), _ = _rounds("col", [partial_value, part_y])
            weight = jnp.sqrt(weight * jnp.sqrt((step_x + 1e-06) / (step_y + 1e-06)))
        tau = (eta / weight)[None, :, None]
        sigma = (eta * weight)[None, :, None]
        new_primal = jnp.clip(primal_reg - tau * (cost_reg - grad), 0.0, upper_reg)
        point = 2.0 * new_primal - primal_reg
        selected = jnp.dot(col_select, point.reshape(region_blocks, width), precision=hp).reshape(
            ntiles, scenarios, lanes
        )
        image = jnp.einsum("tij,tsj->tsi", tiles, selected, precision=hp)
        product = jnp.dot(row_live.T, image.reshape(ntiles, width), precision=hp).reshape(
            row_blocks, scenarios, lanes
        )
        new_dual = jnp.maximum(dual + sigma * (rhs[:, None, :] - product), 0.0)
        local_x = jnp.sum((new_primal - primal_reg) ** 2, axis=(0, 2))
        local_y = jnp.sum((new_dual - dual) ** 2, axis=(0, 2))
        primal_reg, dual = (new_primal, new_dual)
    (step_x, part_y), _ = _rounds("region", [local_x, local_y])
    (step_y,), _ = _rounds("col", [part_y])
    weight = jnp.sqrt(weight * jnp.sqrt((step_x + 1e-06) / (step_y + 1e-06)))
    primal_out = lax.dynamic_slice_in_dim(primal_reg, me * own_blocks, own_blocks, axis=0)
    return (primal_out, dual, weight)


def solution(mesh):
    placed = (
        P(("region", "col"), None, None),
        P(("region", "col")),
        P(("region", "col")),
        P(("region", "col")),
        P(("region", "col"), None),
        P(("region", "col"), None),
        P(("region", "col"), None),
        P(("region", "col"), None, None),
        P(("region", "col"), None, None),
        P(),
        P(),
    )
    return jax.shard_map(
        local,
        mesh=mesh,
        in_specs=placed,
        out_specs=(P(("region", "col"), None, None), P(("region", "col"), None, None), P()),
        check_vma=False,
    )
```

```python
import jax
import jax.numpy as jnp
from jax import lax
from jax.sharding import PartitionSpec as P

ITERS = 2


def _pow2(n):
    return n >= 1 and (n & (n - 1)) == 0


def _exchange(x, axis, n, bit):
    return lax.ppermute(x, axis, [(i, i ^ (1 << bit)) for i in range(n)])


def _rounds(axis, sums, own=None):
    n = lax.axis_size(axis)
    if not _pow2(n):
        sums = [lax.psum(s, axis) for s in sums]
        if own is not None:
            own = lax.all_gather(own, axis, axis=0, tiled=False)
        return sums, own
    shapes = [s.shape for s in sums]
    sizes = [s.size for s in sums]
    me = lax.axis_index(axis)
    buf = None
    if own is not None:
        buf = jnp.zeros((n,) + own.shape, own.dtype)
        buf = lax.dynamic_update_index_in_dim(buf, own, me, 0)
    for bit in range(n.bit_length() - 1):
        parts = [s.reshape(-1) for s in sums]
        if buf is not None:
            used = sum(sizes)
            if used % 1024:
                parts.append(jnp.zeros((-used % 1024,), jnp.float32))
            start = (me >> bit) << bit
            parts.append(lax.dynamic_slice_in_dim(buf, start, 1 << bit, axis=0).reshape(-1))
        flat = jnp.concatenate(parts) if len(parts) > 1 else parts[0]
        got = _exchange(flat, axis, n, bit)
        off = 0
        new_sums = []
        for shape, size, s in zip(shapes, sizes, sums):
            new_sums.append(s + got[off : off + size].reshape(shape))
            off += size
        sums = new_sums
        if buf is not None:
            off += -off % 1024
            theirs = ((me ^ (1 << bit)) >> bit) << bit
            chunk = got[off:].reshape((1 << bit,) + own.shape)
            buf = lax.dynamic_update_slice_in_dim(buf, chunk, theirs, axis=0)
    return sums, buf


def local(
    tiles,
    tile_rows,
    tile_cols,
    tile_count,
    rhs,
    base_cost,
    upper,
    primal,
    dual,
    price_levels,
    scenario_ids,
):
    hp = lax.Precision.HIGHEST
    ntiles = tiles.shape[0]
    row_blocks = rhs.shape[0]
    own_blocks = base_cost.shape[0]
    scenarios = primal.shape[1]
    lanes = primal.shape[2]
    ncol = lax.axis_size("col")
    region_blocks = own_blocks * ncol
    devices = lax.axis_size(("region", "col"))
    me = lax.axis_index("col")
    live = (jnp.arange(ntiles, dtype=jnp.int32) < tile_count[0]).astype(jnp.float32)
    row_select = (tile_rows[:, None] == jnp.arange(row_blocks, dtype=jnp.int32)[None, :]).astype(
        jnp.float32
    )
    row_live = row_select * live[:, None]
    col_select = (tile_cols[:, None] == jnp.arange(region_blocks, dtype=jnp.int32)[None, :]).astype(
        jnp.float32
    )
    col_live = col_select * live[:, None]
    choose = (
        scenario_ids[:, None] == jnp.arange(price_levels.shape[0], dtype=jnp.int32)[None, :]
    ).astype(jnp.float32)
    factor = jnp.dot(choose, price_levels, precision=hp)
    cost = base_cost[:, None, :] * factor[None, :, :]
    local_a = jnp.sum(jnp.sum(tiles * tiles, axis=(1, 2)) * live)
    local_c = jnp.sum(cost * cost, axis=(0, 2))
    local_b = jnp.sum(rhs * rhs)
    width = scenarios * lanes

    def transposed_product(dual):
        dual_rows = jnp.dot(row_select, dual.reshape(row_blocks, width), precision=hp).reshape(
            ntiles, scenarios, lanes
        )
        contrib = jnp.einsum("tij,tsi->tsj", tiles, dual_rows, precision=hp)
        return jnp.dot(col_live.T, contrib.reshape(ntiles, width), precision=hp).reshape(
            region_blocks, scenarios, lanes
        )

    own_rows = own_blocks * (scenarios + 2)
    own = jnp.concatenate(
        [
            primal.reshape(own_blocks * scenarios, lanes),
            base_cost,
            upper,
            jnp.zeros((-own_rows % 8, lanes), jnp.float32),
        ],
        axis=0,
    )
    _, gathered = _rounds("col", [], own)
    gathered, local_a, local_c, local_b = lax.optimization_barrier(
        (gathered, local_a, local_c, local_b)
    )
    (local_a, local_c, local_b), _ = _rounds(
        "region", [local_a.reshape(1), local_c, local_b.reshape(1)]
    )
    partial_value = transposed_product(dual)
    (grad, sq_a, sq_c, sq_b), _ = _rounds("col", [partial_value, local_a, local_c, local_b])
    primal_reg = gathered[:, : own_blocks * scenarios].reshape(region_blocks, scenarios, lanes)
    base_reg = gathered[:, own_blocks * scenarios : own_blocks * (scenarios + 1)]
    upper_reg = gathered[:, own_blocks * (scenarios + 1) : own_rows]
    cost_reg = base_reg.reshape(region_blocks, lanes)[:, None, :] * factor[None, :, :]
    upper_reg = upper_reg.reshape(region_blocks, lanes)[:, None, :]
    eta = 0.5 / jnp.sqrt(sq_a[0] / (lanes * row_blocks * devices))
    weight = jnp.sqrt(sq_c) / jnp.sqrt(sq_b[0])
    for step in range(ITERS):
        if step > 0:
            (step_x, part_y), _ = _rounds("region", [local_x, local_y])
            partial_value = transposed_product(dual)
            (grad, step_y), _ = _rounds("col", [partial_value, part_y])
            weight = jnp.sqrt(weight * jnp.sqrt((step_x + 1e-06) / (step_y + 1e-06)))
        tau = (eta / weight)[None, :, None]
        sigma = (eta * weight)[None, :, None]
        new_primal = jnp.clip(primal_reg - tau * (cost_reg - grad), 0.0, upper_reg)
        point = 2.0 * new_primal - primal_reg
        selected = jnp.dot(col_select, point.reshape(region_blocks, width), precision=hp).reshape(
            ntiles, scenarios, lanes
        )
        image = jnp.einsum("tij,tsj->tsi", tiles, selected, precision=hp)
        product = jnp.dot(row_live.T, image.reshape(ntiles, width), precision=hp).reshape(
            row_blocks, scenarios, lanes
        )
        new_dual = jnp.maximum(dual + sigma * (rhs[:, None, :] - product), 0.0)
        local_x = jnp.sum((new_primal - primal_reg) ** 2, axis=(0, 2))
        local_y = jnp.sum((new_dual - dual) ** 2, axis=(0, 2))
        primal_reg, dual = (new_primal, new_dual)
    (step_x, part_y), _ = _rounds("region", [local_x, local_y])
    (step_y,), _ = _rounds("col", [part_y])
    weight = jnp.sqrt(weight * jnp.sqrt((step_x + 1e-06) / (step_y + 1e-06)))
    primal_out = lax.dynamic_slice_in_dim(primal_reg, me * own_blocks, own_blocks, axis=0)
    return (primal_out, dual, weight)


def solution(mesh):
    placed = (
        P(("region", "col"), None, None),
        P(("region", "col")),
        P(("region", "col")),
        P(("region", "col")),
        P(("region", "col"), None),
        P(("region", "col"), None),
        P(("region", "col"), None),
        P(("region", "col"), None, None),
        P(("region", "col"), None, None),
        P(),
        P(),
    )
    return jax.shard_map(
        local,
        mesh=mesh,
        in_specs=placed,
        out_specs=(P(("region", "col"), None, None), P(("region", "col"), None, None), P()),
        check_vma=False,
    )
```

```python
import jax
import jax.numpy as jnp
from jax import lax
from jax.sharding import PartitionSpec as P

ITERS = 2


def _pow2(n):
    return n >= 1 and (n & (n - 1)) == 0


def _exchange(x, axis, n, bit):
    return lax.ppermute(x, axis, [(i, i ^ (1 << bit)) for i in range(n)])


def _rounds(axis, sums, own=None):
    n = lax.axis_size(axis)
    if not _pow2(n):
        sums = [lax.psum(s, axis) for s in sums]
        if own is not None:
            own = lax.all_gather(own, axis, axis=0, tiled=False)
        return sums, own
    shapes = [s.shape for s in sums]
    sizes = [s.size for s in sums]
    me = lax.axis_index(axis)
    buf = None
    if own is not None:
        buf = jnp.zeros((n,) + own.shape, own.dtype)
        buf = lax.dynamic_update_index_in_dim(buf, own, me, 0)
    for bit in range(n.bit_length() - 1):
        parts = [s.reshape(-1) for s in sums]
        if buf is not None:
            used = sum(sizes)
            parts.append(jnp.zeros((-used % 1024,), jnp.float32))
            start = (me >> bit) << bit
            parts.append(lax.dynamic_slice_in_dim(buf, start, 1 << bit, axis=0).reshape(-1))
        flat = jnp.concatenate(parts) if len(parts) > 1 else parts[0]
        got = _exchange(flat, axis, n, bit)
        off = 0
        new_sums = []
        for shape, size, s in zip(shapes, sizes, sums):
            new_sums.append(s + got[off : off + size].reshape(shape))
            off += size
        sums = new_sums
        if buf is not None:
            off += -off % 1024
            theirs = ((me ^ (1 << bit)) >> bit) << bit
            chunk = got[off:].reshape((1 << bit,) + own.shape)
            buf = lax.dynamic_update_slice_in_dim(buf, chunk, theirs, axis=0)
    return sums, buf


def local(
    tiles,
    tile_rows,
    tile_cols,
    tile_count,
    rhs,
    base_cost,
    upper,
    primal,
    dual,
    price_levels,
    scenario_ids,
):
    hp = lax.Precision.HIGHEST
    ntiles = tiles.shape[0]
    row_blocks = rhs.shape[0]
    own_blocks = base_cost.shape[0]
    scenarios = primal.shape[1]
    lanes = primal.shape[2]
    ncol = lax.axis_size("col")
    region_blocks = own_blocks * ncol
    devices = lax.axis_size(("region", "col"))
    me = lax.axis_index("col")
    live = (jnp.arange(ntiles, dtype=jnp.int32) < tile_count[0]).astype(jnp.float32)
    row_select = (tile_rows[:, None] == jnp.arange(row_blocks, dtype=jnp.int32)[None, :]).astype(
        jnp.float32
    )
    row_live = row_select * live[:, None]
    col_select = (tile_cols[:, None] == jnp.arange(region_blocks, dtype=jnp.int32)[None, :]).astype(
        jnp.float32
    )
    col_live = col_select * live[:, None]
    choose = (
        scenario_ids[:, None] == jnp.arange(price_levels.shape[0], dtype=jnp.int32)[None, :]
    ).astype(jnp.float32)
    factor = jnp.dot(choose, price_levels, precision=hp)
    cost = base_cost[:, None, :] * factor[None, :, :]
    local_a = jnp.sum(jnp.sum(tiles * tiles, axis=(1, 2)) * live)
    local_c = jnp.sum(cost * cost, axis=(0, 2))
    local_b = jnp.sum(rhs * rhs)
    width = scenarios * lanes

    def transposed_product(dual):
        dual_rows = jnp.dot(row_select, dual.reshape(row_blocks, width), precision=hp).reshape(
            ntiles, scenarios, lanes
        )
        contrib = jnp.einsum("tij,tsi->tsj", tiles, dual_rows, precision=hp)
        return jnp.dot(col_live.T, contrib.reshape(ntiles, width), precision=hp).reshape(
            region_blocks, scenarios, lanes
        )

    (local_a, local_c, local_b), _ = _rounds(
        "region", [local_a.reshape(1), local_c, local_b.reshape(1)]
    )
    def placed(x):
        slot = jnp.zeros((region_blocks,) + x.shape[1:], x.dtype)
        return lax.dynamic_update_slice_in_dim(slot, x, me * own_blocks, axis=0)

    partial_value = transposed_product(dual)
    (grad, primal_reg, base_reg, upper_reg, sq_a, sq_c, sq_b), _ = _rounds(
        "col",
        [
            partial_value,
            placed(primal),
            placed(base_cost),
            placed(upper),
            local_a,
            local_c,
            local_b,
        ],
    )
    cost_reg = base_reg[:, None, :] * factor[None, :, :]
    upper_reg = upper_reg[:, None, :]
    eta = 0.5 / jnp.sqrt(sq_a[0] / (lanes * row_blocks * devices))
    weight = jnp.sqrt(sq_c) / jnp.sqrt(sq_b[0])
    for step in range(ITERS):
        if step > 0:
            (step_x, part_y), _ = _rounds("region", [local_x, local_y])
            partial_value = transposed_product(dual)
            (grad, step_y), _ = _rounds("col", [partial_value, part_y])
            weight = jnp.sqrt(weight * jnp.sqrt((step_x + 1e-06) / (step_y + 1e-06)))
        tau = (eta / weight)[None, :, None]
        sigma = (eta * weight)[None, :, None]
        new_primal = jnp.clip(primal_reg - tau * (cost_reg - grad), 0.0, upper_reg)
        point = 2.0 * new_primal - primal_reg
        selected = jnp.dot(col_select, point.reshape(region_blocks, width), precision=hp).reshape(
            ntiles, scenarios, lanes
        )
        image = jnp.einsum("tij,tsj->tsi", tiles, selected, precision=hp)
        product = jnp.dot(row_live.T, image.reshape(ntiles, width), precision=hp).reshape(
            row_blocks, scenarios, lanes
        )
        new_dual = jnp.maximum(dual + sigma * (rhs[:, None, :] - product), 0.0)
        local_x = jnp.sum((new_primal - primal_reg) ** 2, axis=(0, 2))
        local_y = jnp.sum((new_dual - dual) ** 2, axis=(0, 2))
        primal_reg, dual = (new_primal, new_dual)
    (step_x, part_y), _ = _rounds("region", [local_x, local_y])
    (step_y,), _ = _rounds("col", [part_y])
    weight = jnp.sqrt(weight * jnp.sqrt((step_x + 1e-06) / (step_y + 1e-06)))
    primal_out = lax.dynamic_slice_in_dim(primal_reg, me * own_blocks, own_blocks, axis=0)
    return (primal_out, dual, weight)


def solution(mesh):
    placed = (
        P(("region", "col"), None, None),
        P(("region", "col")),
        P(("region", "col")),
        P(("region", "col")),
        P(("region", "col"), None),
        P(("region", "col"), None),
        P(("region", "col"), None),
        P(("region", "col"), None, None),
        P(("region", "col"), None, None),
        P(),
        P(),
    )
    return jax.shard_map(
        local,
        mesh=mesh,
        in_specs=placed,
        out_specs=(P(("region", "col"), None, None), P(("region", "col"), None, None), P()),
        check_vma=False,
    )
```

```python
import jax
import jax.numpy as jnp
from jax import lax
from jax.sharding import PartitionSpec as P

ITERS = 2


def _pow2(n):
    return n >= 1 and (n & (n - 1)) == 0


def _exchange(x, axis, n, bit):
    return lax.ppermute(x, axis, [(i, i ^ (1 << bit)) for i in range(n)])


def _rounds(axis, sums, own=None):
    n = lax.axis_size(axis)
    if not _pow2(n):
        sums = [lax.psum(s, axis) for s in sums]
        if own is not None:
            own = lax.all_gather(own, axis, axis=0, tiled=False)
        return sums, own
    shapes = [s.shape for s in sums]
    sizes = [s.size for s in sums]
    me = lax.axis_index(axis)
    buf = None
    if own is not None:
        buf = jnp.zeros((n,) + own.shape, own.dtype)
        buf = lax.dynamic_update_index_in_dim(buf, own, me, 0)
    for bit in range(n.bit_length() - 1):
        parts = [s.reshape(-1) for s in sums]
        if buf is not None:
            used = sum(sizes)
            if used % 1024:
                parts.append(jnp.zeros((-used % 1024,), jnp.float32))
            start = (me >> bit) << bit
            parts.append(lax.dynamic_slice_in_dim(buf, start, 1 << bit, axis=0).reshape(-1))
        flat = jnp.concatenate(parts) if len(parts) > 1 else parts[0]
        got = _exchange(flat, axis, n, bit)
        off = 0
        new_sums = []
        for shape, size, s in zip(shapes, sizes, sums):
            new_sums.append(s + got[off : off + size].reshape(shape))
            off += size
        sums = new_sums
        if buf is not None:
            off += -off % 1024
            theirs = ((me ^ (1 << bit)) >> bit) << bit
            chunk = got[off:].reshape((1 << bit,) + own.shape)
            buf = lax.dynamic_update_slice_in_dim(buf, chunk, theirs, axis=0)
    return sums, buf


def local(
    tiles,
    tile_rows,
    tile_cols,
    tile_count,
    rhs,
    base_cost,
    upper,
    primal,
    dual,
    price_levels,
    scenario_ids,
):
    hp = lax.Precision.HIGHEST
    ntiles = tiles.shape[0]
    row_blocks = rhs.shape[0]
    own_blocks = base_cost.shape[0]
    scenarios = primal.shape[1]
    lanes = primal.shape[2]
    ncol = lax.axis_size("col")
    region_blocks = own_blocks * ncol
    devices = lax.axis_size(("region", "col"))
    me = lax.axis_index("col")
    live = (jnp.arange(ntiles, dtype=jnp.int32) < tile_count[0]).astype(jnp.float32)
    row_select = (tile_rows[:, None] == jnp.arange(row_blocks, dtype=jnp.int32)[None, :]).astype(
        jnp.float32
    )
    row_live = row_select * live[:, None]
    col_select = (tile_cols[:, None] == jnp.arange(region_blocks, dtype=jnp.int32)[None, :]).astype(
        jnp.float32
    )
    col_live = col_select * live[:, None]
    choose = (
        scenario_ids[:, None] == jnp.arange(price_levels.shape[0], dtype=jnp.int32)[None, :]
    ).astype(jnp.float32)
    factor = jnp.dot(choose, price_levels, precision=hp)
    cost = base_cost[:, None, :] * factor[None, :, :]
    local_a = jnp.sum(jnp.sum(tiles * tiles, axis=(1, 2)) * live)
    local_c = jnp.sum(cost * cost, axis=(0, 2))
    local_b = jnp.sum(rhs * rhs)
    width = scenarios * lanes

    def transposed_product(dual):
        dual_rows = jnp.dot(row_select, dual.reshape(row_blocks, width), precision=hp).reshape(
            ntiles, scenarios, lanes
        )
        contrib = jnp.einsum("tij,tsi->tsj", tiles, dual_rows, precision=hp)
        return jnp.dot(col_live.T, contrib.reshape(ntiles, width), precision=hp).reshape(
            region_blocks, scenarios, lanes
        )

    own_rows = own_blocks * (scenarios + 2)
    own = jnp.concatenate(
        [
            primal.reshape(own_blocks * scenarios, lanes),
            base_cost,
            upper,
            jnp.zeros((-own_rows % 8, lanes), jnp.float32),
        ],
        axis=0,
    )
    _, gathered = _rounds("col", [], own)
    gathered, local_a, local_c, local_b = lax.optimization_barrier(
        (gathered, local_a, local_c, local_b)
    )
    (local_a, local_c, local_b), _ = _rounds(
        "region", [local_a.reshape(1), local_c, local_b.reshape(1)]
    )
    primal_reg = gathered[:, : own_blocks * scenarios].reshape(region_blocks, scenarios, lanes)
    base_reg = gathered[:, own_blocks * scenarios : own_blocks * (scenarios + 1)]
    upper_reg = gathered[:, own_blocks * (scenarios + 1) : own_rows]
    cost_reg = base_reg.reshape(region_blocks, lanes)[:, None, :] * factor[None, :, :]
    upper_reg = jnp.broadcast_to(
        upper_reg.reshape(region_blocks, lanes)[:, None, :], (region_blocks, scenarios, lanes)
    )
    partial_value = transposed_product(dual)
    partial_value, primal_reg, cost_reg, upper_reg = lax.optimization_barrier(
        (partial_value, primal_reg, cost_reg, upper_reg)
    )
    (grad, sq_a, sq_c, sq_b), _ = _rounds("col", [partial_value, local_a, local_c, local_b])
    eta = 0.5 / jnp.sqrt(sq_a[0] / (lanes * row_blocks * devices))
    weight = jnp.sqrt(sq_c) / jnp.sqrt(sq_b[0])
    for step in range(ITERS):
        if step > 0:
            (step_x, part_y), _ = _rounds("region", [local_x, local_y])
            partial_value = transposed_product(dual)
            (grad, step_y), _ = _rounds("col", [partial_value, part_y])
            weight = jnp.sqrt(weight * jnp.sqrt((step_x + 1e-06) / (step_y + 1e-06)))
        tau = (eta / weight)[None, :, None]
        sigma = (eta * weight)[None, :, None]
        new_primal = jnp.clip(primal_reg - tau * (cost_reg - grad), 0.0, upper_reg)
        point = 2.0 * new_primal - primal_reg
        selected = jnp.dot(col_select, point.reshape(region_blocks, width), precision=hp).reshape(
            ntiles, scenarios, lanes
        )
        image = jnp.einsum("tij,tsj->tsi", tiles, selected, precision=hp)
        product = jnp.dot(row_live.T, image.reshape(ntiles, width), precision=hp).reshape(
            row_blocks, scenarios, lanes
        )
        new_dual = jnp.maximum(dual + sigma * (rhs[:, None, :] - product), 0.0)
        local_x = jnp.sum((new_primal - primal_reg) ** 2, axis=(0, 2))
        local_y = jnp.sum((new_dual - dual) ** 2, axis=(0, 2))
        primal_reg, dual = (new_primal, new_dual)
    (step_x, part_y), _ = _rounds("region", [local_x, local_y])
    (step_y,), _ = _rounds("col", [part_y])
    weight = jnp.sqrt(weight * jnp.sqrt((step_x + 1e-06) / (step_y + 1e-06)))
    primal_out = lax.dynamic_slice_in_dim(primal_reg, me * own_blocks, own_blocks, axis=0)
    return (primal_out, dual, weight)


def solution(mesh):
    placed = (
        P(("region", "col"), None, None),
        P(("region", "col")),
        P(("region", "col")),
        P(("region", "col")),
        P(("region", "col"), None),
        P(("region", "col"), None),
        P(("region", "col"), None),
        P(("region", "col"), None, None),
        P(("region", "col"), None, None),
        P(),
        P(),
    )
    return jax.shard_map(
        local,
        mesh=mesh,
        in_specs=placed,
        out_specs=(P(("region", "col"), None, None), P(("region", "col"), None, None), P()),
        check_vma=False,
    )
```

```python
import jax
import jax.numpy as jnp
from jax import lax
from jax.sharding import PartitionSpec as P

ITERS = 2


def _pow2(n):
    return n >= 1 and (n & (n - 1)) == 0


def _exchange(x, axis, n, bit):
    return lax.ppermute(x, axis, [(i, i ^ (1 << bit)) for i in range(n)])


def _rounds(axis, sums, own=None):
    n = lax.axis_size(axis)
    if not _pow2(n):
        sums = [lax.psum(s, axis) for s in sums]
        if own is not None:
            own = lax.all_gather(own, axis, axis=0, tiled=False)
        return sums, own
    shapes = [s.shape for s in sums]
    sizes = [s.size for s in sums]
    me = lax.axis_index(axis)
    buf = None
    if own is not None:
        buf = jnp.zeros((n,) + own.shape, own.dtype)
        buf = lax.dynamic_update_index_in_dim(buf, own, me, 0)
    for bit in range(n.bit_length() - 1):
        parts = [s.reshape(-1) for s in sums]
        if buf is not None:
            used = sum(sizes)
            parts.append(jnp.zeros((-used % 1024,), jnp.float32))
            start = (me >> bit) << bit
            parts.append(lax.dynamic_slice_in_dim(buf, start, 1 << bit, axis=0).reshape(-1))
        flat = jnp.concatenate(parts) if len(parts) > 1 else parts[0]
        got = _exchange(flat, axis, n, bit)
        off = 0
        new_sums = []
        for shape, size, s in zip(shapes, sizes, sums):
            new_sums.append(s + got[off : off + size].reshape(shape))
            off += size
        sums = new_sums
        if buf is not None:
            off += -off % 1024
            theirs = ((me ^ (1 << bit)) >> bit) << bit
            chunk = got[off:].reshape((1 << bit,) + own.shape)
            buf = lax.dynamic_update_slice_in_dim(buf, chunk, theirs, axis=0)
    return sums, buf


def local(
    tiles,
    tile_rows,
    tile_cols,
    tile_count,
    rhs,
    base_cost,
    upper,
    primal,
    dual,
    price_levels,
    scenario_ids,
):
    hp = lax.Precision.HIGHEST
    ntiles = tiles.shape[0]
    row_blocks = rhs.shape[0]
    own_blocks = base_cost.shape[0]
    scenarios = primal.shape[1]
    lanes = primal.shape[2]
    ncol = lax.axis_size("col")
    region_blocks = own_blocks * ncol
    devices = lax.axis_size(("region", "col"))
    me = lax.axis_index("col")
    live = (jnp.arange(ntiles, dtype=jnp.int32) < tile_count[0]).astype(jnp.float32)
    choose = (
        scenario_ids[:, None] == jnp.arange(price_levels.shape[0], dtype=jnp.int32)[None, :]
    ).astype(jnp.float32)
    factor = jnp.dot(choose, price_levels, precision=hp)
    cost = base_cost[:, None, :] * factor[None, :, :]
    local_a = jnp.sum(jnp.sum(tiles * tiles, axis=(1, 2)) * live)
    local_c = jnp.sum(cost * cost, axis=(0, 2))
    local_b = jnp.sum(rhs * rhs)
    width = scenarios * lanes

    place = tile_cols * row_blocks + tile_rows
    place_live = (
        place[None, :] == jnp.arange(region_blocks * row_blocks, dtype=jnp.int32)[:, None]
    ).astype(jnp.float32) * live[None, :]
    dense = jnp.dot(place_live, tiles.reshape(ntiles, -1), precision=hp)
    dense = dense.reshape(region_blocks, row_blocks, tiles.shape[1], tiles.shape[2])
    dense = dense.transpose(1, 2, 0, 3)

    def transposed_product(dual):
        return jnp.einsum("rsi,ricj->csj", dual, dense, precision=hp)

    def product_of(point):
        return jnp.einsum("ricj,csj->rsi", dense, point, precision=hp)

    (local_a, local_c, local_b), _ = _rounds(
        "region", [local_a.reshape(1), local_c, local_b.reshape(1)]
    )
    own_rows = own_blocks * (scenarios + 2)
    own = jnp.concatenate(
        [
            primal.reshape(own_blocks * scenarios, lanes),
            base_cost,
            upper,
            jnp.zeros((-own_rows % 8, lanes), jnp.float32),
        ],
        axis=0,
    )
    partial_value = transposed_product(dual)
    (grad, sq_a, sq_c, sq_b), gathered = _rounds(
        "col", [partial_value, local_a, local_c, local_b], own
    )
    primal_reg = gathered[:, : own_blocks * scenarios].reshape(region_blocks, scenarios, lanes)
    base_reg = gathered[:, own_blocks * scenarios : own_blocks * (scenarios + 1)]
    upper_reg = gathered[:, own_blocks * (scenarios + 1) : own_rows]
    cost_reg = base_reg.reshape(region_blocks, lanes)[:, None, :] * factor[None, :, :]
    upper_reg = upper_reg.reshape(region_blocks, lanes)[:, None, :]
    eta = 0.5 / jnp.sqrt(sq_a[0] / (lanes * row_blocks * devices))
    weight = jnp.sqrt(sq_c) / jnp.sqrt(sq_b[0])
    for step in range(ITERS):
        if step > 0:
            (step_x, part_y), _ = _rounds("region", [local_x, local_y])
            partial_value = transposed_product(dual)
            (grad, step_y), _ = _rounds("col", [partial_value, part_y])
            weight = jnp.sqrt(weight * jnp.sqrt((step_x + 1e-06) / (step_y + 1e-06)))
        tau = (eta / weight)[None, :, None]
        sigma = (eta * weight)[None, :, None]
        new_primal = jnp.clip(primal_reg - tau * (cost_reg - grad), 0.0, upper_reg)
        point = 2.0 * new_primal - primal_reg
        product = product_of(point)
        new_dual = jnp.maximum(dual + sigma * (rhs[:, None, :] - product), 0.0)
        local_x = jnp.sum((new_primal - primal_reg) ** 2, axis=(0, 2))
        local_y = jnp.sum((new_dual - dual) ** 2, axis=(0, 2))
        primal_reg, dual = (new_primal, new_dual)
    (step_x, part_y), _ = _rounds("region", [local_x, local_y])
    (step_y,), _ = _rounds("col", [part_y])
    weight = jnp.sqrt(weight * jnp.sqrt((step_x + 1e-06) / (step_y + 1e-06)))
    primal_out = lax.dynamic_slice_in_dim(primal_reg, me * own_blocks, own_blocks, axis=0)
    return (primal_out, dual, weight)


def solution(mesh):
    placed = (
        P(("region", "col"), None, None),
        P(("region", "col")),
        P(("region", "col")),
        P(("region", "col")),
        P(("region", "col"), None),
        P(("region", "col"), None),
        P(("region", "col"), None),
        P(("region", "col"), None, None),
        P(("region", "col"), None, None),
        P(),
        P(),
    )
    return jax.shard_map(
        local,
        mesh=mesh,
        in_specs=placed,
        out_specs=(P(("region", "col"), None, None), P(("region", "col"), None, None), P()),
        check_vma=False,
    )
```

```python
import jax
import jax.numpy as jnp
from jax import lax
from jax.sharding import PartitionSpec as P

ITERS = 2


def _pow2(n):
    return n >= 1 and (n & (n - 1)) == 0


def _exchange(x, axis, n, bit):
    return lax.ppermute(x, axis, [(i, i ^ (1 << bit)) for i in range(n)])


def _rounds(axis, sums, own=None, split=None):
    n = lax.axis_size(axis)
    if split is not None and (not _pow2(n) or n < 2 or split.shape[0] % 2):
        sums = [split] + list(sums)
        split = None
        joined = True
    else:
        joined = False
    if not _pow2(n):
        sums = [lax.psum(s, axis) for s in sums]
        if own is not None:
            own = lax.all_gather(own, axis, axis=0, tiled=False)
        return (sums[0] if joined else None), sums[1:] if joined else sums, own
    shapes = [s.shape for s in sums]
    sizes = [s.size for s in sums]
    me = lax.axis_index(axis)
    buf = None
    if own is not None:
        buf = jnp.zeros((n,) + own.shape, own.dtype)
        buf = lax.dynamic_update_index_in_dim(buf, own, me, 0)
    if split is not None:
        half = lax.rem(me, 2)
        halves = split.reshape((2, split.shape[0] // 2) + split.shape[1:])
        keep = lax.dynamic_index_in_dim(halves, half, 0, keepdims=False)
        give = lax.dynamic_index_in_dim(halves, 1 - half, 0, keepdims=False)
    for bit in range(n.bit_length() - 1):
        parts = []
        if split is not None:
            parts.append((give if bit == 0 else keep).reshape(-1))
        parts += [s.reshape(-1) for s in sums]
        if buf is not None:
            used = sum(p.shape[0] for p in parts)
            if used % 1024:
                parts.append(jnp.zeros((-used % 1024,), jnp.float32))
            start = (me >> bit) << bit
            parts.append(lax.dynamic_slice_in_dim(buf, start, 1 << bit, axis=0).reshape(-1))
        flat = jnp.concatenate(parts) if len(parts) > 1 else parts[0]
        got = _exchange(flat, axis, n, bit)
        off = 0
        if split is not None:
            keep = keep + got[: keep.size].reshape(keep.shape)
            off = keep.size
        new_sums = []
        for shape, size, s in zip(shapes, sizes, sums):
            new_sums.append(s + got[off : off + size].reshape(shape))
            off += size
        sums = new_sums
        if buf is not None:
            off += -off % 1024
            theirs = ((me ^ (1 << bit)) >> bit) << bit
            chunk = got[off:].reshape((1 << bit,) + own.shape)
            buf = lax.dynamic_update_slice_in_dim(buf, chunk, theirs, axis=0)
    full = None
    if split is not None:
        other = _exchange(keep, axis, n, 0)
        both = jnp.concatenate([keep, other, keep], axis=0)
        full = lax.dynamic_slice_in_dim(both, half * keep.shape[0], 2 * keep.shape[0], axis=0)
    elif joined:
        full, sums = sums[0], sums[1:]
    return full, sums, buf


def local(
    tiles,
    tile_rows,
    tile_cols,
    tile_count,
    rhs,
    base_cost,
    upper,
    primal,
    dual,
    price_levels,
    scenario_ids,
):
    hp = lax.Precision.HIGHEST
    ntiles = tiles.shape[0]
    row_blocks = rhs.shape[0]
    own_blocks = base_cost.shape[0]
    scenarios = primal.shape[1]
    lanes = primal.shape[2]
    ncol = lax.axis_size("col")
    region_blocks = own_blocks * ncol
    devices = lax.axis_size(("region", "col"))
    me = lax.axis_index("col")
    live = (jnp.arange(ntiles, dtype=jnp.int32) < tile_count[0]).astype(jnp.float32)
    choose = (
        scenario_ids[:, None] == jnp.arange(price_levels.shape[0], dtype=jnp.int32)[None, :]
    ).astype(jnp.float32)
    factor = jnp.dot(choose, price_levels, precision=hp)
    cost = base_cost[:, None, :] * factor[None, :, :]
    local_a = jnp.sum(jnp.sum(tiles * tiles, axis=(1, 2)) * live)
    local_c = jnp.sum(cost * cost, axis=(0, 2))
    local_b = jnp.sum(rhs * rhs)
    width = scenarios * lanes

    place = tile_cols * row_blocks + tile_rows
    place_live = (
        place[None, :] == jnp.arange(region_blocks * row_blocks, dtype=jnp.int32)[:, None]
    ).astype(jnp.float32) * live[None, :]
    dense = jnp.dot(place_live, tiles.reshape(ntiles, -1), precision=hp)
    dense = dense.reshape(region_blocks, row_blocks, tiles.shape[1], tiles.shape[2])
    dense = dense.transpose(1, 2, 0, 3)

    def transposed_product(dual):
        return jnp.einsum("rsi,ricj->csj", dual, dense, precision=hp)

    def product_of(point):
        return jnp.einsum("ricj,csj->rsi", dense, point, precision=hp)

    _, (local_a, local_c, local_b), _ = _rounds(
        "region", [local_a.reshape(1), local_c, local_b.reshape(1)]
    )
    own_rows = own_blocks * (scenarios + 2)
    own = jnp.concatenate(
        [
            primal.reshape(own_blocks * scenarios, lanes),
            base_cost,
            upper,
            jnp.zeros((-own_rows % 8, lanes), jnp.float32),
        ],
        axis=0,
    )
    partial_value = transposed_product(dual)
    grad, (sq_a, sq_c, sq_b), gathered = _rounds(
        "col", [local_a, local_c, local_b], own, split=partial_value
    )
    primal_reg = gathered[:, : own_blocks * scenarios].reshape(region_blocks, scenarios, lanes)
    base_reg = gathered[:, own_blocks * scenarios : own_blocks * (scenarios + 1)]
    upper_reg = gathered[:, own_blocks * (scenarios + 1) : own_rows]
    cost_reg = base_reg.reshape(region_blocks, lanes)[:, None, :] * factor[None, :, :]
    upper_reg = upper_reg.reshape(region_blocks, lanes)[:, None, :]
    eta = 0.5 / jnp.sqrt(sq_a[0] / (lanes * row_blocks * devices))
    weight = jnp.sqrt(sq_c) / jnp.sqrt(sq_b[0])
    for step in range(ITERS):
        if step > 0:
            _, (step_x, part_y), _ = _rounds("region", [local_x, local_y])
            partial_value = transposed_product(dual)
            grad, (step_y,), _ = _rounds("col", [part_y], split=partial_value)
            weight = jnp.sqrt(weight * jnp.sqrt((step_x + 1e-06) / (step_y + 1e-06)))
        tau = (eta / weight)[None, :, None]
        sigma = (eta * weight)[None, :, None]
        new_primal = jnp.clip(primal_reg - tau * (cost_reg - grad), 0.0, upper_reg)
        point = 2.0 * new_primal - primal_reg
        product = product_of(point)
        new_dual = jnp.maximum(dual + sigma * (rhs[:, None, :] - product), 0.0)
        local_x = jnp.sum((new_primal - primal_reg) ** 2, axis=(0, 2))
        local_y = jnp.sum((new_dual - dual) ** 2, axis=(0, 2))
        primal_reg, dual = (new_primal, new_dual)
    _, (step_x, part_y), _ = _rounds("region", [local_x, local_y])
    _, (step_y,), _ = _rounds("col", [part_y])
    weight = jnp.sqrt(weight * jnp.sqrt((step_x + 1e-06) / (step_y + 1e-06)))
    primal_out = lax.dynamic_slice_in_dim(primal_reg, me * own_blocks, own_blocks, axis=0)
    return (primal_out, dual, weight)


def solution(mesh):
    placed = (
        P(("region", "col"), None, None),
        P(("region", "col")),
        P(("region", "col")),
        P(("region", "col")),
        P(("region", "col"), None),
        P(("region", "col"), None),
        P(("region", "col"), None),
        P(("region", "col"), None, None),
        P(("region", "col"), None, None),
        P(),
        P(),
    )
    return jax.shard_map(
        local,
        mesh=mesh,
        in_specs=placed,
        out_specs=(P(("region", "col"), None, None), P(("region", "col"), None, None), P()),
        check_vma=False,
    )
```

```python
import jax
import jax.numpy as jnp
from jax import lax
from jax.sharding import PartitionSpec as P

ITERS = 2


def _pow2(n):
    return n >= 1 and (n & (n - 1)) == 0


def _exchange(x, axis, n, bit):
    return lax.ppermute(x, axis, [(i, i ^ (1 << bit)) for i in range(n)])


def _rounds(axis, sums, own=None, split=None):
    n = lax.axis_size(axis)
    if split is not None and (not _pow2(n) or n < 2 or split.shape[0] % 2):
        sums = [split] + list(sums)
        split = None
        joined = True
    else:
        joined = False
    if not _pow2(n):
        sums = [lax.psum(s, axis) for s in sums]
        if own is not None:
            own = lax.all_gather(own, axis, axis=0, tiled=False)
        return (sums[0] if joined else None), sums[1:] if joined else sums, own
    shapes = [s.shape for s in sums]
    sizes = [s.size for s in sums]
    me = lax.axis_index(axis)
    buf = None
    if own is not None:
        buf = jnp.zeros((n,) + own.shape, own.dtype)
        buf = lax.dynamic_update_index_in_dim(buf, own, me, 0)
    if split is not None:
        half = lax.rem(me, 2)
        halves = split.reshape((2, split.shape[0] // 2) + split.shape[1:])
        keep = lax.dynamic_index_in_dim(halves, half, 0, keepdims=False)
        give = lax.dynamic_index_in_dim(halves, 1 - half, 0, keepdims=False)
    for bit in range(n.bit_length() - 1):
        parts = []
        if split is not None:
            parts.append((give if bit == 0 else keep).reshape(-1))
        parts += [s.reshape(-1) for s in sums]
        if buf is not None:
            used = sum(p.shape[0] for p in parts)
            if used % 1024:
                parts.append(jnp.zeros((-used % 1024,), jnp.float32))
            start = (me >> bit) << bit
            parts.append(lax.dynamic_slice_in_dim(buf, start, 1 << bit, axis=0).reshape(-1))
        flat = jnp.concatenate(parts) if len(parts) > 1 else parts[0]
        got = _exchange(flat, axis, n, bit)
        off = 0
        if split is not None:
            keep = keep + got[: keep.size].reshape(keep.shape)
            off = keep.size
        new_sums = []
        for shape, size, s in zip(shapes, sizes, sums):
            new_sums.append(s + got[off : off + size].reshape(shape))
            off += size
        sums = new_sums
        if buf is not None:
            off += -off % 1024
            theirs = ((me ^ (1 << bit)) >> bit) << bit
            chunk = got[off:].reshape((1 << bit,) + own.shape)
            buf = lax.dynamic_update_slice_in_dim(buf, chunk, theirs, axis=0)
    full = None
    if split is not None:
        other = _exchange(keep, axis, n, 0)
        both = jnp.concatenate([keep, other, keep], axis=0)
        full = lax.dynamic_slice_in_dim(both, half * keep.shape[0], 2 * keep.shape[0], axis=0)
    elif joined:
        full, sums = sums[0], sums[1:]
    return full, sums, buf


def local(
    tiles,
    tile_rows,
    tile_cols,
    tile_count,
    rhs,
    base_cost,
    upper,
    primal,
    dual,
    price_levels,
    scenario_ids,
):
    hp = lax.Precision.HIGHEST
    ntiles = tiles.shape[0]
    row_blocks = rhs.shape[0]
    own_blocks = base_cost.shape[0]
    scenarios = primal.shape[1]
    lanes = primal.shape[2]
    ncol = lax.axis_size("col")
    region_blocks = own_blocks * ncol
    devices = lax.axis_size(("region", "col"))
    me = lax.axis_index("col")
    live = (jnp.arange(ntiles, dtype=jnp.int32) < tile_count[0]).astype(jnp.float32)
    choose = (
        scenario_ids[:, None] == jnp.arange(price_levels.shape[0], dtype=jnp.int32)[None, :]
    ).astype(jnp.float32)
    factor = jnp.dot(choose, price_levels, precision=hp)
    cost = base_cost[:, None, :] * factor[None, :, :]
    local_a = jnp.sum(jnp.sum(tiles * tiles, axis=(1, 2)) * live)
    local_c = jnp.sum(cost * cost, axis=(0, 2))
    local_b = jnp.sum(rhs * rhs)
    width = scenarios * lanes

    place = tile_cols * row_blocks + tile_rows
    place_live = (
        place[None, :] == jnp.arange(region_blocks * row_blocks, dtype=jnp.int32)[:, None]
    ).astype(jnp.float32) * live[None, :]
    dense = jnp.dot(place_live, tiles.reshape(ntiles, -1), precision=hp)
    dense = dense.reshape(region_blocks, row_blocks, tiles.shape[1], tiles.shape[2])
    dense = dense.transpose(1, 2, 0, 3)

    def transposed_product(dual):
        return jnp.einsum("rsi,ricj->csj", dual, dense, precision=hp)

    def product_of(point):
        return jnp.einsum("ricj,csj->rsi", dense, point, precision=hp)

    own_rows = own_blocks * (scenarios + 2)
    own = jnp.concatenate(
        [
            primal.reshape(own_blocks * scenarios, lanes),
            base_cost,
            upper,
            jnp.zeros((-own_rows % 8, lanes), jnp.float32),
        ],
        axis=0,
    )
    _, _, gathered = _rounds("col", [], own)
    gathered, local_a, local_c, local_b = lax.optimization_barrier(
        (gathered, local_a, local_c, local_b)
    )
    _, (local_a, local_c, local_b), _ = _rounds(
        "region", [local_a.reshape(1), local_c, local_b.reshape(1)]
    )
    primal_reg = gathered[:, : own_blocks * scenarios].reshape(region_blocks, scenarios, lanes)
    base_reg = gathered[:, own_blocks * scenarios : own_blocks * (scenarios + 1)]
    upper_reg = gathered[:, own_blocks * (scenarios + 1) : own_rows]
    cost_reg = base_reg.reshape(region_blocks, lanes)[:, None, :] * factor[None, :, :]
    upper_reg = jnp.broadcast_to(
        upper_reg.reshape(region_blocks, lanes)[:, None, :], (region_blocks, scenarios, lanes)
    )
    partial_value = transposed_product(dual)
    partial_value, primal_reg, cost_reg, upper_reg = lax.optimization_barrier(
        (partial_value, primal_reg, cost_reg, upper_reg)
    )
    grad, (sq_a, sq_c, sq_b), _ = _rounds(
        "col", [local_a, local_c, local_b], split=partial_value
    )
    eta = 0.5 / jnp.sqrt(sq_a[0] / (lanes * row_blocks * devices))
    weight = jnp.sqrt(sq_c) / jnp.sqrt(sq_b[0])
    for step in range(ITERS):
        if step > 0:
            _, (step_x, part_y), _ = _rounds("region", [local_x, local_y])
            partial_value = transposed_product(dual)
            grad, (step_y,), _ = _rounds("col", [part_y], split=partial_value)
            weight = jnp.sqrt(weight * jnp.sqrt((step_x + 1e-06) / (step_y + 1e-06)))
        tau = (eta / weight)[None, :, None]
        sigma = (eta * weight)[None, :, None]
        new_primal = jnp.clip(primal_reg - tau * (cost_reg - grad), 0.0, upper_reg)
        point = 2.0 * new_primal - primal_reg
        product = product_of(point)
        new_dual = jnp.maximum(dual + sigma * (rhs[:, None, :] - product), 0.0)
        local_x = jnp.sum((new_primal - primal_reg) ** 2, axis=(0, 2))
        local_y = jnp.sum((new_dual - dual) ** 2, axis=(0, 2))
        primal_reg, dual = (new_primal, new_dual)
    _, (step_x, part_y), _ = _rounds("region", [local_x, local_y])
    _, (step_y,), _ = _rounds("col", [part_y])
    weight = jnp.sqrt(weight * jnp.sqrt((step_x + 1e-06) / (step_y + 1e-06)))
    primal_out = lax.dynamic_slice_in_dim(primal_reg, me * own_blocks, own_blocks, axis=0)
    return (primal_out, dual, weight)


def solution(mesh):
    placed = (
        P(("region", "col"), None, None),
        P(("region", "col")),
        P(("region", "col")),
        P(("region", "col")),
        P(("region", "col"), None),
        P(("region", "col"), None),
        P(("region", "col"), None),
        P(("region", "col"), None, None),
        P(("region", "col"), None, None),
        P(),
        P(),
    )
    return jax.shard_map(
        local,
        mesh=mesh,
        in_specs=placed,
        out_specs=(P(("region", "col"), None, None), P(("region", "col"), None, None), P()),
        check_vma=False,
    )
```

```python
import jax
import jax.numpy as jnp
from jax import lax
from jax.sharding import PartitionSpec as P

ITERS = 2


def _pow2(n):
    return n >= 1 and (n & (n - 1)) == 0


def _exchange(x, axis, n, bit):
    return lax.ppermute(x, axis, [(i, i ^ (1 << bit)) for i in range(n)])


def _rounds(axis, sums, own=None, split=None):
    n = lax.axis_size(axis)
    if split is not None and (not _pow2(n) or n < 2 or split.shape[0] % 2):
        sums = [split] + list(sums)
        split = None
        joined = True
    else:
        joined = False
    if not _pow2(n):
        sums = [lax.psum(s, axis) for s in sums]
        if own is not None:
            own = lax.all_gather(own, axis, axis=0, tiled=False)
        return (sums[0] if joined else None), sums[1:] if joined else sums, own
    shapes = [s.shape for s in sums]
    sizes = [s.size for s in sums]
    me = lax.axis_index(axis)
    buf = None
    if own is not None:
        buf = jnp.zeros((n,) + own.shape, own.dtype)
        buf = lax.dynamic_update_index_in_dim(buf, own, me, 0)
    if split is not None:
        half = lax.rem(me, 2)
        halves = split.reshape((2, split.shape[0] // 2) + split.shape[1:])
        keep = lax.dynamic_index_in_dim(halves, half, 0, keepdims=False)
        give = lax.dynamic_index_in_dim(halves, 1 - half, 0, keepdims=False)
    for bit in range(n.bit_length() - 1):
        parts = []
        if split is not None:
            parts.append((give if bit == 0 else keep).reshape(-1))
        parts += [s.reshape(-1) for s in sums]
        if buf is not None:
            used = sum(p.shape[0] for p in parts)
            if used % 1024:
                parts.append(jnp.zeros((-used % 1024,), jnp.float32))
            start = (me >> bit) << bit
            parts.append(lax.dynamic_slice_in_dim(buf, start, 1 << bit, axis=0).reshape(-1))
        flat = jnp.concatenate(parts) if len(parts) > 1 else parts[0]
        got = _exchange(flat, axis, n, bit)
        off = 0
        if split is not None:
            keep = keep + got[: keep.size].reshape(keep.shape)
            off = keep.size
        new_sums = []
        for shape, size, s in zip(shapes, sizes, sums):
            new_sums.append(s + got[off : off + size].reshape(shape))
            off += size
        sums = new_sums
        if buf is not None:
            off += -off % 1024
            theirs = ((me ^ (1 << bit)) >> bit) << bit
            chunk = got[off:].reshape((1 << bit,) + own.shape)
            buf = lax.dynamic_update_slice_in_dim(buf, chunk, theirs, axis=0)
    full = None
    if split is not None:
        other = _exchange(keep, axis, n, 0)
        both = jnp.concatenate([keep, other, keep], axis=0)
        full = lax.dynamic_slice_in_dim(both, half * keep.shape[0], 2 * keep.shape[0], axis=0)
    elif joined:
        full, sums = sums[0], sums[1:]
    return full, sums, buf


def local(
    tiles,
    tile_rows,
    tile_cols,
    tile_count,
    rhs,
    base_cost,
    upper,
    primal,
    dual,
    price_levels,
    scenario_ids,
):
    hp = lax.Precision.HIGHEST
    ntiles = tiles.shape[0]
    row_blocks = rhs.shape[0]
    own_blocks = base_cost.shape[0]
    scenarios = primal.shape[1]
    lanes = primal.shape[2]
    ncol = lax.axis_size("col")
    region_blocks = own_blocks * ncol
    devices = lax.axis_size(("region", "col"))
    me = lax.axis_index("col")
    live = (jnp.arange(ntiles, dtype=jnp.int32) < tile_count[0]).astype(jnp.float32)
    choose = (
        scenario_ids[:, None] == jnp.arange(price_levels.shape[0], dtype=jnp.int32)[None, :]
    ).astype(jnp.float32)
    factor = jnp.dot(choose, price_levels, precision=hp)
    cost = base_cost[:, None, :] * factor[None, :, :]
    local_a = jnp.sum(jnp.sum(tiles * tiles, axis=(1, 2)) * live)
    local_c = jnp.sum(cost * cost, axis=(0, 2))
    local_b = jnp.sum(rhs * rhs)
    width = scenarios * lanes

    place = tile_cols * row_blocks + tile_rows
    place_live = (
        place[None, :] == jnp.arange(region_blocks * row_blocks, dtype=jnp.int32)[:, None]
    ).astype(jnp.float32) * live[None, :]
    dense = jnp.dot(place_live, tiles.reshape(ntiles, -1), precision=hp)
    dense = dense.reshape(region_blocks, row_blocks, tiles.shape[1], tiles.shape[2])
    dense = dense.transpose(1, 2, 0, 3)

    def transposed_product(dual):
        return jnp.einsum("rsi,ricj->csj", dual, dense, precision=lax.Precision.HIGH)

    def product_of(point):
        return jnp.einsum("ricj,csj->rsi", dense, point, precision=lax.Precision.HIGH)

    _, (local_a, local_c, local_b), _ = _rounds(
        "region", [local_a.reshape(1), local_c, local_b.reshape(1)]
    )
    own_rows = own_blocks * (scenarios + 2)
    own = jnp.concatenate(
        [
            primal.reshape(own_blocks * scenarios, lanes),
            base_cost,
            upper,
            jnp.zeros((-own_rows % 8, lanes), jnp.float32),
        ],
        axis=0,
    )
    partial_value = transposed_product(dual)
    grad, (sq_a, sq_c, sq_b), gathered = _rounds(
        "col", [local_a, local_c, local_b], own, split=partial_value
    )
    primal_reg = gathered[:, : own_blocks * scenarios].reshape(region_blocks, scenarios, lanes)
    base_reg = gathered[:, own_blocks * scenarios : own_blocks * (scenarios + 1)]
    upper_reg = gathered[:, own_blocks * (scenarios + 1) : own_rows]
    cost_reg = base_reg.reshape(region_blocks, lanes)[:, None, :] * factor[None, :, :]
    upper_reg = upper_reg.reshape(region_blocks, lanes)[:, None, :]
    eta = 0.5 / jnp.sqrt(sq_a[0] / (lanes * row_blocks * devices))
    weight = jnp.sqrt(sq_c) / jnp.sqrt(sq_b[0])
    for step in range(ITERS):
        if step > 0:
            _, (step_x, part_y), _ = _rounds("region", [local_x, local_y])
            partial_value = transposed_product(dual)
            grad, (step_y,), _ = _rounds("col", [part_y], split=partial_value)
            weight = jnp.sqrt(weight * jnp.sqrt((step_x + 1e-06) / (step_y + 1e-06)))
        tau = (eta / weight)[None, :, None]
        sigma = (eta * weight)[None, :, None]
        new_primal = jnp.clip(primal_reg - tau * (cost_reg - grad), 0.0, upper_reg)
        point = 2.0 * new_primal - primal_reg
        product = product_of(point)
        new_dual = jnp.maximum(dual + sigma * (rhs[:, None, :] - product), 0.0)
        local_x = jnp.sum((new_primal - primal_reg) ** 2, axis=(0, 2))
        local_y = jnp.sum((new_dual - dual) ** 2, axis=(0, 2))
        primal_reg, dual = (new_primal, new_dual)
    _, (step_x, part_y), _ = _rounds("region", [local_x, local_y])
    _, (step_y,), _ = _rounds("col", [part_y])
    weight = jnp.sqrt(weight * jnp.sqrt((step_x + 1e-06) / (step_y + 1e-06)))
    primal_out = lax.dynamic_slice_in_dim(primal_reg, me * own_blocks, own_blocks, axis=0)
    return (primal_out, dual, weight)


def solution(mesh):
    placed = (
        P(("region", "col"), None, None),
        P(("region", "col")),
        P(("region", "col")),
        P(("region", "col")),
        P(("region", "col"), None),
        P(("region", "col"), None),
        P(("region", "col"), None),
        P(("region", "col"), None, None),
        P(("region", "col"), None, None),
        P(),
        P(),
    )
    return jax.shard_map(
        local,
        mesh=mesh,
        in_specs=placed,
        out_specs=(P(("region", "col"), None, None), P(("region", "col"), None, None), P()),
        check_vma=False,
    )
```

```python
import jax
import jax.numpy as jnp
from jax import lax
from jax.sharding import PartitionSpec as P

ITERS = 2


def _pow2(n):
    return n >= 1 and (n & (n - 1)) == 0


def _exchange(x, axis, n, bit):
    return lax.ppermute(x, axis, [(i, i ^ (1 << bit)) for i in range(n)])


def _rounds(axis, sums, own=None, split=None):
    n = lax.axis_size(axis)
    if split is not None and (not _pow2(n) or n < 2 or split.shape[0] % 2):
        sums = [split] + list(sums)
        split = None
        joined = True
    else:
        joined = False
    if not _pow2(n):
        sums = [lax.psum(s, axis) for s in sums]
        if own is not None:
            own = lax.all_gather(own, axis, axis=0, tiled=False)
        return (sums[0] if joined else None), sums[1:] if joined else sums, own
    shapes = [s.shape for s in sums]
    sizes = [s.size for s in sums]
    me = lax.axis_index(axis)
    buf = None
    if own is not None:
        buf = jnp.zeros((n,) + own.shape, own.dtype)
        buf = lax.dynamic_update_index_in_dim(buf, own, me, 0)
    if split is not None:
        half = lax.rem(me, 2)
        halves = split.reshape((2, split.shape[0] // 2) + split.shape[1:])
        keep = lax.dynamic_index_in_dim(halves, half, 0, keepdims=False)
        give = lax.dynamic_index_in_dim(halves, 1 - half, 0, keepdims=False)
    for bit in range(n.bit_length() - 1):
        parts = []
        if split is not None:
            parts.append((give if bit == 0 else keep).reshape(-1))
        parts += [s.reshape(-1) for s in sums]
        if buf is not None:
            used = sum(p.shape[0] for p in parts)
            if used % 1024:
                parts.append(jnp.zeros((-used % 1024,), jnp.float32))
            start = (me >> bit) << bit
            parts.append(lax.dynamic_slice_in_dim(buf, start, 1 << bit, axis=0).reshape(-1))
        flat = jnp.concatenate(parts) if len(parts) > 1 else parts[0]
        got = _exchange(flat, axis, n, bit)
        off = 0
        if split is not None:
            keep = keep + got[: keep.size].reshape(keep.shape)
            off = keep.size
        new_sums = []
        for shape, size, s in zip(shapes, sizes, sums):
            new_sums.append(s + got[off : off + size].reshape(shape))
            off += size
        sums = new_sums
        if buf is not None:
            off += -off % 1024
            theirs = ((me ^ (1 << bit)) >> bit) << bit
            chunk = got[off:].reshape((1 << bit,) + own.shape)
            buf = lax.dynamic_update_slice_in_dim(buf, chunk, theirs, axis=0)
    full = None
    if split is not None:
        other = _exchange(keep, axis, n, 0)
        both = jnp.concatenate([keep, other, keep], axis=0)
        full = lax.dynamic_slice_in_dim(both, half * keep.shape[0], 2 * keep.shape[0], axis=0)
    elif joined:
        full, sums = sums[0], sums[1:]
    return full, sums, buf


def local(
    tiles,
    tile_rows,
    tile_cols,
    tile_count,
    rhs,
    base_cost,
    upper,
    primal,
    dual,
    price_levels,
    scenario_ids,
):
    hp = lax.Precision.HIGHEST
    ntiles = tiles.shape[0]
    row_blocks = rhs.shape[0]
    own_blocks = base_cost.shape[0]
    scenarios = primal.shape[1]
    lanes = primal.shape[2]
    ncol = lax.axis_size("col")
    region_blocks = own_blocks * ncol
    devices = lax.axis_size(("region", "col"))
    me = lax.axis_index("col")
    live = (jnp.arange(ntiles, dtype=jnp.int32) < tile_count[0]).astype(jnp.float32)
    choose = (
        scenario_ids[:, None] == jnp.arange(price_levels.shape[0], dtype=jnp.int32)[None, :]
    ).astype(jnp.float32)
    factor = jnp.dot(choose, price_levels, precision=hp)
    cost = base_cost[:, None, :] * factor[None, :, :]
    local_a = jnp.sum(jnp.sum(tiles * tiles, axis=(1, 2)) * live)
    local_c = jnp.sum(cost * cost, axis=(0, 2))
    local_b = jnp.sum(rhs * rhs)
    width = scenarios * lanes

    place = tile_cols * row_blocks + tile_rows
    place_live = (
        place[None, :] == jnp.arange(region_blocks * row_blocks, dtype=jnp.int32)[:, None]
    ).astype(jnp.float32) * live[None, :]
    dense = jnp.dot(place_live, tiles.reshape(ntiles, -1), precision=hp)
    dense = dense.reshape(region_blocks, row_blocks, tiles.shape[1], tiles.shape[2])
    dense = dense.transpose(1, 2, 0, 3)

    def transposed_product(dual):
        return jnp.einsum("rsi,ricj->csj", dual, dense, precision=lax.Precision.HIGH)

    def product_of(point):
        return jnp.einsum("ricj,csj->rsi", dense, point, precision=lax.Precision.HIGH)

    _, (local_a, local_c, local_b), _ = _rounds(
        "region", [local_a.reshape(1), local_c, local_b.reshape(1)]
    )
    own_rows = own_blocks * (scenarios + 2)
    own = jnp.concatenate(
        [
            primal.reshape(own_blocks * scenarios, lanes),
            base_cost,
            upper,
            jnp.zeros((-own_rows % 8, lanes), jnp.float32),
        ],
        axis=0,
    )
    partial_value = transposed_product(dual)
    _, (sq_a, sq_c, sq_b), _ = _rounds("col", [local_a, local_c, local_b])
    grad, _, gathered = _rounds("col", [], own, split=partial_value)
    primal_reg = gathered[:, : own_blocks * scenarios].reshape(region_blocks, scenarios, lanes)
    base_reg = gathered[:, own_blocks * scenarios : own_blocks * (scenarios + 1)]
    upper_reg = gathered[:, own_blocks * (scenarios + 1) : own_rows]
    cost_reg = base_reg.reshape(region_blocks, lanes)[:, None, :] * factor[None, :, :]
    upper_reg = upper_reg.reshape(region_blocks, lanes)[:, None, :]
    eta = 0.5 / jnp.sqrt(sq_a[0] / (lanes * row_blocks * devices))
    weight = jnp.sqrt(sq_c) / jnp.sqrt(sq_b[0])
    for step in range(ITERS):
        if step > 0:
            _, (step_x, part_y), _ = _rounds("region", [local_x, local_y])
            _, (step_y,), _ = _rounds("col", [part_y])
            partial_value = transposed_product(dual)
            grad, _, _ = _rounds("col", [], split=partial_value)
            weight = jnp.sqrt(weight * jnp.sqrt((step_x + 1e-06) / (step_y + 1e-06)))
        tau = (eta / weight)[None, :, None]
        sigma = (eta * weight)[None, :, None]
        new_primal = jnp.clip(primal_reg - tau * (cost_reg - grad), 0.0, upper_reg)
        point = 2.0 * new_primal - primal_reg
        product = product_of(point)
        new_dual = jnp.maximum(dual + sigma * (rhs[:, None, :] - product), 0.0)
        local_x = jnp.sum((new_primal - primal_reg) ** 2, axis=(0, 2))
        local_y = jnp.sum((new_dual - dual) ** 2, axis=(0, 2))
        primal_reg, dual = (new_primal, new_dual)
    _, (step_x, part_y), _ = _rounds("region", [local_x, local_y])
    _, (step_y,), _ = _rounds("col", [part_y])
    weight = jnp.sqrt(weight * jnp.sqrt((step_x + 1e-06) / (step_y + 1e-06)))
    primal_out = lax.dynamic_slice_in_dim(primal_reg, me * own_blocks, own_blocks, axis=0)
    return (primal_out, dual, weight)


def solution(mesh):
    placed = (
        P(("region", "col"), None, None),
        P(("region", "col")),
        P(("region", "col")),
        P(("region", "col")),
        P(("region", "col"), None),
        P(("region", "col"), None),
        P(("region", "col"), None),
        P(("region", "col"), None, None),
        P(("region", "col"), None, None),
        P(),
        P(),
    )
    return jax.shard_map(
        local,
        mesh=mesh,
        in_specs=placed,
        out_specs=(P(("region", "col"), None, None), P(("region", "col"), None, None), P()),
        check_vma=False,
    )
```

```python
import jax
import jax.numpy as jnp
from jax import lax
from jax.sharding import PartitionSpec as P

ITERS = 2


def _pow2(n):
    return n >= 1 and (n & (n - 1)) == 0


def _exchange(x, axis, n, bit):
    return lax.ppermute(x, axis, [(i, i ^ (1 << bit)) for i in range(n)])


def _rounds(axis, sums, own=None, split=None):
    n = lax.axis_size(axis)
    if split is not None and (not _pow2(n) or n < 2 or split.shape[0] % 2):
        sums = [split] + list(sums)
        split = None
        joined = True
    else:
        joined = False
    if not _pow2(n):
        sums = [lax.psum(s, axis) for s in sums]
        if own is not None:
            own = lax.all_gather(own, axis, axis=0, tiled=False)
        return (sums[0] if joined else None), sums[1:] if joined else sums, own
    shapes = [s.shape for s in sums]
    sizes = [s.size for s in sums]
    me = lax.axis_index(axis)
    buf = None
    if own is not None:
        buf = jnp.zeros((n,) + own.shape, own.dtype)
        buf = lax.dynamic_update_index_in_dim(buf, own, me, 0)
    if split is not None:
        half = lax.rem(me, 2)
        halves = split.reshape((2, split.shape[0] // 2) + split.shape[1:])
        keep = lax.dynamic_index_in_dim(halves, half, 0, keepdims=False)
        give = lax.dynamic_index_in_dim(halves, 1 - half, 0, keepdims=False)
    for bit in range(n.bit_length() - 1):
        parts = []
        if split is not None:
            parts.append((give if bit == 0 else keep).reshape(-1))
        parts += [s.reshape(-1) for s in sums]
        if buf is not None:
            used = sum(p.shape[0] for p in parts)
            if used % 1024:
                parts.append(jnp.zeros((-used % 1024,), jnp.float32))
            start = (me >> bit) << bit
            parts.append(lax.dynamic_slice_in_dim(buf, start, 1 << bit, axis=0).reshape(-1))
        flat = jnp.concatenate(parts) if len(parts) > 1 else parts[0]
        got = _exchange(flat, axis, n, bit)
        off = 0
        if split is not None:
            keep = keep + got[: keep.size].reshape(keep.shape)
            off = keep.size
        new_sums = []
        for shape, size, s in zip(shapes, sizes, sums):
            new_sums.append(s + got[off : off + size].reshape(shape))
            off += size
        sums = new_sums
        if buf is not None:
            off += -off % 1024
            theirs = ((me ^ (1 << bit)) >> bit) << bit
            chunk = got[off:].reshape((1 << bit,) + own.shape)
            buf = lax.dynamic_update_slice_in_dim(buf, chunk, theirs, axis=0)
    full = None
    if split is not None:
        other = _exchange(keep, axis, n, 0)
        both = jnp.concatenate([keep, other, keep], axis=0)
        full = lax.dynamic_slice_in_dim(both, half * keep.shape[0], 2 * keep.shape[0], axis=0)
    elif joined:
        full, sums = sums[0], sums[1:]
    return full, sums, buf


def local(
    tiles,
    tile_rows,
    tile_cols,
    tile_count,
    rhs,
    base_cost,
    upper,
    primal,
    dual,
    price_levels,
    scenario_ids,
):
    hp = lax.Precision.HIGHEST
    ntiles = tiles.shape[0]
    row_blocks = rhs.shape[0]
    own_blocks = base_cost.shape[0]
    scenarios = primal.shape[1]
    lanes = primal.shape[2]
    ncol = lax.axis_size("col")
    region_blocks = own_blocks * ncol
    devices = lax.axis_size(("region", "col"))
    me = lax.axis_index("col")
    live = (jnp.arange(ntiles, dtype=jnp.int32) < tile_count[0]).astype(jnp.float32)
    choose = (
        scenario_ids[:, None] == jnp.arange(price_levels.shape[0], dtype=jnp.int32)[None, :]
    ).astype(jnp.float32)
    factor = jnp.dot(choose, price_levels, precision=hp)
    cost = base_cost[:, None, :] * factor[None, :, :]
    local_a = jnp.sum(jnp.sum(tiles * tiles * live[:, None, None], axis=(0, 1)))
    local_c = jnp.sum(cost * cost, axis=(0, 2))
    local_b = jnp.sum(rhs * rhs)
    width = scenarios * lanes

    place = tile_cols * row_blocks + tile_rows
    place_live = (
        place[None, :] == jnp.arange(region_blocks * row_blocks, dtype=jnp.int32)[:, None]
    ).astype(jnp.float32) * live[None, :]
    dense = jnp.dot(place_live, tiles.reshape(ntiles, -1), precision=hp)
    dense = dense.reshape(region_blocks, row_blocks, tiles.shape[1], tiles.shape[2])
    dense = dense.transpose(1, 2, 0, 3)

    def transposed_product(dual):
        return jnp.einsum("rsi,ricj->csj", dual, dense, precision=lax.Precision.HIGH)

    def product_of(point):
        return jnp.einsum("ricj,csj->rsi", dense, point, precision=lax.Precision.HIGH)

    _, (local_a, local_c, local_b), _ = _rounds(
        "region", [local_a.reshape(1), local_c, local_b.reshape(1)]
    )
    own_rows = own_blocks * (scenarios + 2)
    own = jnp.concatenate(
        [
            primal.reshape(own_blocks * scenarios, lanes),
            base_cost,
            upper,
            jnp.zeros((-own_rows % 8, lanes), jnp.float32),
        ],
        axis=0,
    )
    partial_value = transposed_product(dual)
    grad, (sq_a, sq_c, sq_b), gathered = _rounds(
        "col", [local_a, local_c, local_b], own, split=partial_value
    )
    primal_reg = gathered[:, : own_blocks * scenarios].reshape(region_blocks, scenarios, lanes)
    base_reg = gathered[:, own_blocks * scenarios : own_blocks * (scenarios + 1)]
    upper_reg = gathered[:, own_blocks * (scenarios + 1) : own_rows]
    cost_reg = base_reg.reshape(region_blocks, lanes)[:, None, :] * factor[None, :, :]
    upper_reg = upper_reg.reshape(region_blocks, lanes)[:, None, :]
    eta = 0.5 / jnp.sqrt(sq_a[0] / (lanes * row_blocks * devices))
    weight = jnp.sqrt(sq_c) / jnp.sqrt(sq_b[0])
    for step in range(ITERS):
        if step > 0:
            _, (step_x, part_y), _ = _rounds("region", [local_x, local_y])
            partial_value = transposed_product(dual)
            grad, (step_y,), _ = _rounds("col", [part_y], split=partial_value)
            weight = jnp.sqrt(weight * jnp.sqrt((step_x + 1e-06) / (step_y + 1e-06)))
        tau = (eta / weight)[None, :, None]
        sigma = (eta * weight)[None, :, None]
        new_primal = jnp.clip(primal_reg - tau * (cost_reg - grad), 0.0, upper_reg)
        point = 2.0 * new_primal - primal_reg
        product = product_of(point)
        new_dual = jnp.maximum(dual + sigma * (rhs[:, None, :] - product), 0.0)
        local_x = jnp.sum((new_primal - primal_reg) ** 2, axis=(0, 2))
        local_y = jnp.sum((new_dual - dual) ** 2, axis=(0, 2))
        primal_reg, dual = (new_primal, new_dual)
    _, (step_x, part_y), _ = _rounds("region", [local_x, local_y])
    _, (step_y,), _ = _rounds("col", [part_y])
    weight = jnp.sqrt(weight * jnp.sqrt((step_x + 1e-06) / (step_y + 1e-06)))
    primal_out = lax.dynamic_slice_in_dim(primal_reg, me * own_blocks, own_blocks, axis=0)
    return (primal_out, dual, weight)


def solution(mesh):
    placed = (
        P(("region", "col"), None, None),
        P(("region", "col")),
        P(("region", "col")),
        P(("region", "col")),
        P(("region", "col"), None),
        P(("region", "col"), None),
        P(("region", "col"), None),
        P(("region", "col"), None, None),
        P(("region", "col"), None, None),
        P(),
        P(),
    )
    return jax.shard_map(
        local,
        mesh=mesh,
        in_specs=placed,
        out_specs=(P(("region", "col"), None, None), P(("region", "col"), None, None), P()),
        check_vma=False,
    )
```

```python
import jax
import jax.numpy as jnp
from jax import lax
from jax.sharding import PartitionSpec as P

ITERS = 2


def _pow2(n):
    return n >= 1 and (n & (n - 1)) == 0


def _exchange(x, axis, n, bit):
    return lax.ppermute(x, axis, [(i, i ^ (1 << bit)) for i in range(n)])


def _gather_order(n):
    bits = n.bit_length() - 1
    return list(range(1, bits)) + [0] if bits > 1 else list(range(bits))


def _slot(index, n):
    out = 0
    for m, bit in enumerate(_gather_order(n)):
        out = out + (((index >> bit) & 1) << m)
    return out


def _rounds(axis, sums, own=None, split=None):
    n = lax.axis_size(axis)
    if not _pow2(n) or n < 2:
        sums = [lax.psum(s, axis) for s in sums]
        full = None if split is None else lax.psum(split, axis)
        if own is not None:
            own = lax.all_gather(own, axis, axis=0, tiled=False)
        return full, sums, own
    shapes = [s.shape for s in sums]
    sizes = [s.size for s in sums]
    me = lax.axis_index(axis)
    order = _gather_order(n)
    bits = n.bit_length() - 1
    buf = None
    if own is not None:
        assert split is not None
        mine_slot = _slot(me, n)
        buf = jnp.zeros((n,) + own.shape, own.dtype)
        buf = lax.dynamic_update_index_in_dim(buf, own, mine_slot, 0)
    if split is not None:
        half = lax.rem(me, 2)
        halves = split.reshape((2, split.shape[0] // 2) + split.shape[1:])
        keep = lax.dynamic_index_in_dim(halves, half, 0, keepdims=False)
        give = lax.dynamic_index_in_dim(halves, 1 - half, 0, keepdims=False)
    steps = list(range(bits)) + ([0] if split is not None else [])
    m = 0
    for step, bit in enumerate(steps):
        last = split is not None and step == bits
        parts = []
        if split is not None:
            parts.append((give if step == 0 else keep).reshape(-1))
        if not last:
            parts += [s.reshape(-1) for s in sums]
        carry = buf is not None and m < bits and order[m] == bit and (step > 0 or bits == 1)
        if carry:
            used = sum(p.shape[0] for p in parts)
            if used % 1024:
                parts.append(jnp.zeros((-used % 1024,), jnp.float32))
            start = (mine_slot >> m) << m
            parts.append(lax.dynamic_slice_in_dim(buf, start, 1 << m, axis=0).reshape(-1))
        flat = jnp.concatenate(parts) if len(parts) > 1 else parts[0]
        got = _exchange(flat, axis, n, bit)
        off = 0
        if split is not None:
            piece = got[: keep.size].reshape(keep.shape)
            if last:
                other = piece
            else:
                keep = keep + piece
            off = keep.size
        if not last:
            new_sums = []
            for shape, size, s in zip(shapes, sizes, sums):
                new_sums.append(s + got[off : off + size].reshape(shape))
                off += size
            sums = new_sums
        if carry:
            off += -off % 1024
            theirs = ((mine_slot ^ (1 << m)) >> m) << m
            chunk = got[off:].reshape((1 << m,) + own.shape)
            buf = lax.dynamic_update_slice_in_dim(buf, chunk, theirs, axis=0)
            m += 1
    full = None
    if split is not None:
        both = jnp.concatenate([keep, other, keep], axis=0)
        full = lax.dynamic_slice_in_dim(both, half * keep.shape[0], 2 * keep.shape[0], axis=0)
    return full, sums, buf


def local(
    tiles,
    tile_rows,
    tile_cols,
    tile_count,
    rhs,
    base_cost,
    upper,
    primal,
    dual,
    price_levels,
    scenario_ids,
):
    hp = lax.Precision.HIGHEST
    ntiles = tiles.shape[0]
    row_blocks = rhs.shape[0]
    own_blocks = base_cost.shape[0]
    scenarios = primal.shape[1]
    lanes = primal.shape[2]
    ncol = lax.axis_size("col")
    region_blocks = own_blocks * ncol
    devices = lax.axis_size(("region", "col"))
    me = lax.axis_index("col")
    live = (jnp.arange(ntiles, dtype=jnp.int32) < tile_count[0]).astype(jnp.float32)
    choose = (
        scenario_ids[:, None] == jnp.arange(price_levels.shape[0], dtype=jnp.int32)[None, :]
    ).astype(jnp.float32)
    factor = jnp.dot(choose, price_levels, precision=hp)
    cost = base_cost[:, None, :] * factor[None, :, :]
    local_a = jnp.sum(jnp.sum(tiles * tiles, axis=(1, 2)) * live)
    local_c = jnp.sum(cost * cost, axis=(0, 2))
    local_b = jnp.sum(rhs * rhs)
    width = scenarios * lanes

    slot_cols = _slot(tile_cols // own_blocks, ncol) * own_blocks + tile_cols % own_blocks
    place = slot_cols * row_blocks + tile_rows
    place_live = (
        place[None, :] == jnp.arange(region_blocks * row_blocks, dtype=jnp.int32)[:, None]
    ).astype(jnp.float32) * live[None, :]
    dense = jnp.dot(place_live, tiles.reshape(ntiles, -1), precision=hp)
    dense = dense.reshape(region_blocks, row_blocks, tiles.shape[1], tiles.shape[2])
    dense = dense.transpose(1, 2, 0, 3)

    def transposed_product(dual):
        return jnp.einsum("rsi,ricj->csj", dual, dense, precision=lax.Precision.HIGH)

    def product_of(point):
        return jnp.einsum("ricj,csj->rsi", dense, point, precision=lax.Precision.HIGH)

    _, (local_a, local_c, local_b), _ = _rounds(
        "region", [local_a.reshape(1), local_c, local_b.reshape(1)]
    )
    own_rows = own_blocks * (scenarios + 2)
    own = jnp.concatenate(
        [
            primal.reshape(own_blocks * scenarios, lanes),
            base_cost,
            upper,
            jnp.zeros((-own_rows % 8, lanes), jnp.float32),
        ],
        axis=0,
    )
    partial_value = transposed_product(dual)
    grad, (sq_a, sq_c, sq_b), gathered = _rounds(
        "col", [local_a, local_c, local_b], own, split=partial_value
    )
    primal_reg = gathered[:, : own_blocks * scenarios].reshape(region_blocks, scenarios, lanes)
    base_reg = gathered[:, own_blocks * scenarios : own_blocks * (scenarios + 1)]
    upper_reg = gathered[:, own_blocks * (scenarios + 1) : own_rows]
    cost_reg = base_reg.reshape(region_blocks, lanes)[:, None, :] * factor[None, :, :]
    upper_reg = upper_reg.reshape(region_blocks, lanes)[:, None, :]
    eta = 0.5 / jnp.sqrt(sq_a[0] / (lanes * row_blocks * devices))
    weight = jnp.sqrt(sq_c) / jnp.sqrt(sq_b[0])
    for step in range(ITERS):
        if step > 0:
            _, (step_x, part_y), _ = _rounds("region", [local_x, local_y])
            partial_value = transposed_product(dual)
            grad, (step_y,), _ = _rounds("col", [part_y], split=partial_value)
            weight = jnp.sqrt(weight * jnp.sqrt((step_x + 1e-06) / (step_y + 1e-06)))
        tau = (eta / weight)[None, :, None]
        sigma = (eta * weight)[None, :, None]
        new_primal = jnp.clip(primal_reg - tau * (cost_reg - grad), 0.0, upper_reg)
        point = 2.0 * new_primal - primal_reg
        product = product_of(point)
        new_dual = jnp.maximum(dual + sigma * (rhs[:, None, :] - product), 0.0)
        local_x = jnp.sum((new_primal - primal_reg) ** 2, axis=(0, 2))
        local_y = jnp.sum((new_dual - dual) ** 2, axis=(0, 2))
        primal_reg, dual = (new_primal, new_dual)
    _, (step_x, part_y), _ = _rounds("region", [local_x, local_y])
    _, (step_y,), _ = _rounds("col", [part_y])
    weight = jnp.sqrt(weight * jnp.sqrt((step_x + 1e-06) / (step_y + 1e-06)))
    primal_out = lax.dynamic_slice_in_dim(
        primal_reg, _slot(me, ncol) * own_blocks, own_blocks, axis=0
    )
    return (primal_out, dual, weight)


def solution(mesh):
    placed = (
        P(("region", "col"), None, None),
        P(("region", "col")),
        P(("region", "col")),
        P(("region", "col")),
        P(("region", "col"), None),
        P(("region", "col"), None),
        P(("region", "col"), None),
        P(("region", "col"), None, None),
        P(("region", "col"), None, None),
        P(),
        P(),
    )
    return jax.shard_map(
        local,
        mesh=mesh,
        in_specs=placed,
        out_specs=(P(("region", "col"), None, None), P(("region", "col"), None, None), P()),
        check_vma=False,
    )
```

```python
import jax
import jax.numpy as jnp
from jax import lax
from jax.sharding import PartitionSpec as P

ITERS = 2


def _pow2(n):
    return n >= 1 and (n & (n - 1)) == 0


def _exchange(x, axis, n, bit):
    return lax.ppermute(x, axis, [(i, i ^ (1 << bit)) for i in range(n)])


def _gather_order(n):
    bits = n.bit_length() - 1
    return list(range(1, bits)) + [0] if bits > 1 else list(range(bits))


def _slot(index, n):
    out = 0
    for m, bit in enumerate(_gather_order(n)):
        out = out + (((index >> bit) & 1) << m)
    return out


def _rounds(axis, sums, own=None, split=None):
    n = lax.axis_size(axis)
    if not _pow2(n) or n < 2:
        sums = [lax.psum(s, axis) for s in sums]
        full = None if split is None else lax.psum(split, axis)
        if own is not None:
            own = lax.all_gather(own, axis, axis=0, tiled=False)
        return full, sums, own
    shapes = [s.shape for s in sums]
    sizes = [s.size for s in sums]
    me = lax.axis_index(axis)
    order = _gather_order(n)
    bits = n.bit_length() - 1
    buf = None
    if own is not None:
        assert split is not None
        mine_slot = _slot(me, n)
        buf = jnp.zeros((n,) + own.shape, own.dtype)
        buf = lax.dynamic_update_index_in_dim(buf, own, mine_slot, 0)
    if split is not None:
        half = lax.rem(me, 2)
        halves = split.reshape((2, split.shape[0] // 2) + split.shape[1:])
        keep = lax.dynamic_index_in_dim(halves, half, 0, keepdims=False)
        give = lax.dynamic_index_in_dim(halves, 1 - half, 0, keepdims=False)
    steps = list(range(bits)) + ([0] if split is not None else [])
    m = 0
    for step, bit in enumerate(steps):
        last = split is not None and step == bits
        parts = []
        if split is not None:
            parts.append((give if step == 0 else keep).reshape(-1))
        if not last:
            parts += [s.reshape(-1) for s in sums]
        carry = buf is not None and m < bits and order[m] == bit and (step > 0 or bits == 1)
        if carry:
            used = sum(p.shape[0] for p in parts)
            if used % 1024:
                parts.append(jnp.zeros((-used % 1024,), jnp.float32))
            start = (mine_slot >> m) << m
            parts.append(lax.dynamic_slice_in_dim(buf, start, 1 << m, axis=0).reshape(-1))
        flat = jnp.concatenate(parts) if len(parts) > 1 else parts[0]
        got = _exchange(flat, axis, n, bit)
        off = 0
        if split is not None:
            piece = got[: keep.size].reshape(keep.shape)
            if last:
                other = piece
            else:
                keep = keep + piece
            off = keep.size
        if not last:
            new_sums = []
            for shape, size, s in zip(shapes, sizes, sums):
                new_sums.append(s + got[off : off + size].reshape(shape))
                off += size
            sums = new_sums
        if carry:
            off += -off % 1024
            theirs = ((mine_slot ^ (1 << m)) >> m) << m
            chunk = got[off:].reshape((1 << m,) + own.shape)
            buf = lax.dynamic_update_slice_in_dim(buf, chunk, theirs, axis=0)
            m += 1
    full = None
    if split is not None:
        both = jnp.concatenate([keep, other, keep], axis=0)
        full = lax.dynamic_slice_in_dim(both, half * keep.shape[0], 2 * keep.shape[0], axis=0)
    return full, sums, buf


def local(
    tiles,
    tile_rows,
    tile_cols,
    tile_count,
    rhs,
    base_cost,
    upper,
    primal,
    dual,
    price_levels,
    scenario_ids,
):
    hp = lax.Precision.HIGHEST
    ntiles = tiles.shape[0]
    row_blocks = rhs.shape[0]
    own_blocks = base_cost.shape[0]
    scenarios = primal.shape[1]
    lanes = primal.shape[2]
    ncol = lax.axis_size("col")
    region_blocks = own_blocks * ncol
    devices = lax.axis_size(("region", "col"))
    me = lax.axis_index("col")
    live = (jnp.arange(ntiles, dtype=jnp.int32) < tile_count[0]).astype(jnp.float32)
    choose = (
        scenario_ids[:, None] == jnp.arange(price_levels.shape[0], dtype=jnp.int32)[None, :]
    ).astype(jnp.float32)
    factor = jnp.dot(choose, price_levels, precision=hp)
    cost = base_cost[:, None, :] * factor[None, :, :]
    local_a = jnp.sum(jnp.sum(tiles * tiles, axis=(1, 2)) * live)
    local_c = jnp.sum(cost * cost, axis=(0, 2))
    local_b = jnp.sum(rhs * rhs)
    width = scenarios * lanes

    slot_cols = _slot(tile_cols // own_blocks, ncol) * own_blocks + tile_cols % own_blocks
    place = slot_cols * row_blocks + tile_rows
    place_live = (
        place[None, :] == jnp.arange(region_blocks * row_blocks, dtype=jnp.int32)[:, None]
    ).astype(jnp.float32) * live[None, :]
    dense = jnp.dot(place_live, tiles.reshape(ntiles, -1), precision=hp)
    dense = dense.reshape(region_blocks, row_blocks, tiles.shape[1], tiles.shape[2])
    dense = dense.transpose(1, 2, 0, 3)

    def transposed_product(dual):
        return jnp.einsum("rsi,ricj->csj", dual, dense, precision=lax.Precision.HIGH)

    def product_of(point):
        return jnp.einsum("ricj,csj->rsi", dense, point, precision=lax.Precision.HIGH)

    norms = jnp.concatenate([local_a.reshape(1), local_c, local_b.reshape(1)])
    _, (norms,), _ = _rounds("region", [norms])
    own_rows = own_blocks * (scenarios + 2)
    own = jnp.concatenate(
        [
            primal.reshape(own_blocks * scenarios, lanes),
            base_cost,
            upper,
            jnp.zeros((-own_rows % 8, lanes), jnp.float32),
        ],
        axis=0,
    )
    partial_value = transposed_product(dual)
    grad, (norms,), gathered = _rounds("col", [norms], own, split=partial_value)
    sq_a, sq_c, sq_b = norms[0], norms[1 : scenarios + 1], norms[scenarios + 1]
    primal_reg = gathered[:, : own_blocks * scenarios].reshape(region_blocks, scenarios, lanes)
    base_reg = gathered[:, own_blocks * scenarios : own_blocks * (scenarios + 1)]
    upper_reg = gathered[:, own_blocks * (scenarios + 1) : own_rows]
    cost_reg = base_reg.reshape(region_blocks, lanes)[:, None, :] * factor[None, :, :]
    upper_reg = upper_reg.reshape(region_blocks, lanes)[:, None, :]
    eta = 0.5 / jnp.sqrt(sq_a / (lanes * row_blocks * devices))
    weight = jnp.sqrt(sq_c) / jnp.sqrt(sq_b)
    for step in range(ITERS):
        if step > 0:
            _, (step_x, part_y), _ = _rounds("region", [local_x, local_y])
            partial_value = transposed_product(dual)
            grad, (step_y,), _ = _rounds("col", [part_y], split=partial_value)
            weight = jnp.sqrt(weight * jnp.sqrt((step_x + 1e-06) / (step_y + 1e-06)))
        tau = (eta / weight)[None, :, None]
        sigma = (eta * weight)[None, :, None]
        new_primal = jnp.clip(primal_reg - tau * (cost_reg - grad), 0.0, upper_reg)
        point = 2.0 * new_primal - primal_reg
        product = product_of(point)
        new_dual = jnp.maximum(dual + sigma * (rhs[:, None, :] - product), 0.0)
        local_x = jnp.sum((new_primal - primal_reg) ** 2, axis=(0, 2))
        local_y = jnp.sum((new_dual - dual) ** 2, axis=(0, 2))
        primal_reg, dual = (new_primal, new_dual)
    _, (step_x, part_y), _ = _rounds("region", [local_x, local_y])
    _, (step_y,), _ = _rounds("col", [part_y])
    weight = jnp.sqrt(weight * jnp.sqrt((step_x + 1e-06) / (step_y + 1e-06)))
    primal_out = lax.dynamic_slice_in_dim(
        primal_reg, _slot(me, ncol) * own_blocks, own_blocks, axis=0
    )
    return (primal_out, dual, weight)


def solution(mesh):
    placed = (
        P(("region", "col"), None, None),
        P(("region", "col")),
        P(("region", "col")),
        P(("region", "col")),
        P(("region", "col"), None),
        P(("region", "col"), None),
        P(("region", "col"), None),
        P(("region", "col"), None, None),
        P(("region", "col"), None, None),
        P(),
        P(),
    )
    return jax.shard_map(
        local,
        mesh=mesh,
        in_specs=placed,
        out_specs=(P(("region", "col"), None, None), P(("region", "col"), None, None), P()),
        check_vma=False,
    )
```

```python
import jax
import jax.numpy as jnp
from jax import lax
from jax.sharding import PartitionSpec as P

ITERS = 2


def _pow2(n):
    return n >= 1 and (n & (n - 1)) == 0


def _exchange(x, axis, n, bit):
    return lax.ppermute(x, axis, [(i, i ^ (1 << bit)) for i in range(n)])


def _gather_order(n):
    bits = n.bit_length() - 1
    return list(range(1, bits)) + [0] if bits > 1 else list(range(bits))


def _slot(index, n):
    out = 0
    for m, bit in enumerate(_gather_order(n)):
        out = out + (((index >> bit) & 1) << m)
    return out


def _rounds(axis, sums, own=None, split=None):
    n = lax.axis_size(axis)
    if not _pow2(n) or n < 2:
        sums = [lax.psum(s, axis) for s in sums]
        full = None if split is None else lax.psum(split, axis)
        if own is not None:
            own = lax.all_gather(own, axis, axis=0, tiled=False)
        return full, sums, own
    shapes = [s.shape for s in sums]
    sizes = [s.size for s in sums]
    me = lax.axis_index(axis)
    order = _gather_order(n)
    bits = n.bit_length() - 1
    buf = None
    if own is not None:
        assert split is not None
        mine_slot = _slot(me, n)
        buf = jnp.zeros((n,) + own.shape, own.dtype)
        buf = lax.dynamic_update_index_in_dim(buf, own, mine_slot, 0)
    if split is not None:
        half = lax.rem(me, 2)
        halves = split.reshape((2, split.shape[0] // 2) + split.shape[1:])
        keep = lax.dynamic_index_in_dim(halves, half, 0, keepdims=False)
        give = lax.dynamic_index_in_dim(halves, 1 - half, 0, keepdims=False)
    steps = list(range(bits)) + ([0] if split is not None else [])
    m = 0
    for step, bit in enumerate(steps):
        last = split is not None and step == bits
        parts = []
        if split is not None:
            parts.append((give if step == 0 else keep).reshape(-1))
        if not last:
            parts += [s.reshape(-1) for s in sums]
        carry = buf is not None and m < bits and order[m] == bit and (step > 0 or bits == 1)
        if carry:
            used = sum(p.shape[0] for p in parts)
            if used % 1024:
                parts.append(jnp.zeros((-used % 1024,), jnp.float32))
            start = (mine_slot >> m) << m
            parts.append(lax.dynamic_slice_in_dim(buf, start, 1 << m, axis=0).reshape(-1))
        flat = jnp.concatenate(parts) if len(parts) > 1 else parts[0]
        got = _exchange(flat, axis, n, bit)
        off = 0
        if split is not None:
            piece = got[: keep.size].reshape(keep.shape)
            if last:
                other = piece
            else:
                keep = keep + piece
            off = keep.size
        if not last:
            new_sums = []
            for shape, size, s in zip(shapes, sizes, sums):
                new_sums.append(s + got[off : off + size].reshape(shape))
                off += size
            sums = new_sums
        if carry:
            off += -off % 1024
            theirs = ((mine_slot ^ (1 << m)) >> m) << m
            chunk = got[off:].reshape((1 << m,) + own.shape)
            buf = lax.dynamic_update_slice_in_dim(buf, chunk, theirs, axis=0)
            m += 1
    full = None
    if split is not None:
        both = jnp.concatenate([keep, other, keep], axis=0)
        full = lax.dynamic_slice_in_dim(both, half * keep.shape[0], 2 * keep.shape[0], axis=0)
    return full, sums, buf


def local(
    tiles,
    tile_rows,
    tile_cols,
    tile_count,
    rhs,
    base_cost,
    upper,
    primal,
    dual,
    price_levels,
    scenario_ids,
):
    hp = lax.Precision.HIGHEST
    ntiles = tiles.shape[0]
    row_blocks = rhs.shape[0]
    own_blocks = base_cost.shape[0]
    scenarios = primal.shape[1]
    lanes = primal.shape[2]
    ncol = lax.axis_size("col")
    region_blocks = own_blocks * ncol
    devices = lax.axis_size(("region", "col"))
    me = lax.axis_index("col")
    live = (jnp.arange(ntiles, dtype=jnp.int32) < tile_count[0]).astype(jnp.float32)
    choose = (
        scenario_ids[:, None] == jnp.arange(price_levels.shape[0], dtype=jnp.int32)[None, :]
    ).astype(jnp.float32)
    factor = jnp.dot(choose, price_levels, precision=hp)
    cost = base_cost[:, None, :] * factor[None, :, :]
    local_a = jnp.sum(jnp.sum(tiles * tiles, axis=(1, 2)) * live)
    local_c = jnp.sum(cost * cost, axis=(0, 2))
    local_b = jnp.sum(rhs * rhs)
    width = scenarios * lanes

    slot_cols = _slot(tile_cols // own_blocks, ncol) * own_blocks + tile_cols % own_blocks
    place = slot_cols * row_blocks + tile_rows
    place_live = (
        place[None, :] == jnp.arange(region_blocks * row_blocks, dtype=jnp.int32)[:, None]
    ).astype(jnp.float32) * live[None, :]

    def transposed_product(dual):
        return jnp.einsum("rsi,ricj->csj", dual, dense, precision=lax.Precision.HIGH)

    def product_of(point):
        return jnp.einsum("ricj,csj->rsi", dense, point, precision=lax.Precision.HIGH)

    norms = jnp.concatenate([local_a.reshape(1), local_c, local_b.reshape(1)])
    n_region = lax.axis_size("region")
    if _pow2(n_region) and n_region >= 2:
        norms = norms + _exchange(norms, "region", n_region, 0)
        norms, place_live = lax.optimization_barrier((norms, place_live))
        for bit in range(1, n_region.bit_length() - 1):
            norms = norms + _exchange(norms, "region", n_region, bit)
    else:
        norms = lax.psum(norms, "region")
    dense = jnp.dot(place_live, tiles.reshape(ntiles, -1), precision=hp)
    dense = dense.reshape(region_blocks, row_blocks, tiles.shape[1], tiles.shape[2])
    dense = dense.transpose(1, 2, 0, 3)
    own_rows = own_blocks * (scenarios + 2)
    own = jnp.concatenate(
        [
            primal.reshape(own_blocks * scenarios, lanes),
            base_cost,
            upper,
            jnp.zeros((-own_rows % 8, lanes), jnp.float32),
        ],
        axis=0,
    )
    partial_value = transposed_product(dual)
    grad, (norms,), gathered = _rounds("col", [norms], own, split=partial_value)
    sq_a, sq_c, sq_b = norms[0], norms[1 : scenarios + 1], norms[scenarios + 1]
    primal_reg = gathered[:, : own_blocks * scenarios].reshape(region_blocks, scenarios, lanes)
    base_reg = gathered[:, own_blocks * scenarios : own_blocks * (scenarios + 1)]
    upper_reg = gathered[:, own_blocks * (scenarios + 1) : own_rows]
    cost_reg = base_reg.reshape(region_blocks, lanes)[:, None, :] * factor[None, :, :]
    upper_reg = upper_reg.reshape(region_blocks, lanes)[:, None, :]
    eta = 0.5 / jnp.sqrt(sq_a / (lanes * row_blocks * devices))
    weight = jnp.sqrt(sq_c) / jnp.sqrt(sq_b)
    for step in range(ITERS):
        if step > 0:
            _, (step_x, part_y), _ = _rounds("region", [local_x, local_y])
            partial_value = transposed_product(dual)
            grad, (step_y,), _ = _rounds("col", [part_y], split=partial_value)
            weight = jnp.sqrt(weight * jnp.sqrt((step_x + 1e-06) / (step_y + 1e-06)))
        tau = (eta / weight)[None, :, None]
        sigma = (eta * weight)[None, :, None]
        new_primal = jnp.clip(primal_reg - tau * (cost_reg - grad), 0.0, upper_reg)
        point = 2.0 * new_primal - primal_reg
        product = product_of(point)
        new_dual = jnp.maximum(dual + sigma * (rhs[:, None, :] - product), 0.0)
        local_x = jnp.sum((new_primal - primal_reg) ** 2, axis=(0, 2))
        local_y = jnp.sum((new_dual - dual) ** 2, axis=(0, 2))
        primal_reg, dual = (new_primal, new_dual)
    _, (step_x, part_y), _ = _rounds("region", [local_x, local_y])
    _, (step_y,), _ = _rounds("col", [part_y])
    weight = jnp.sqrt(weight * jnp.sqrt((step_x + 1e-06) / (step_y + 1e-06)))
    primal_out = lax.dynamic_slice_in_dim(
        primal_reg, _slot(me, ncol) * own_blocks, own_blocks, axis=0
    )
    return (primal_out, dual, weight)


def solution(mesh):
    placed = (
        P(("region", "col"), None, None),
        P(("region", "col")),
        P(("region", "col")),
        P(("region", "col")),
        P(("region", "col"), None),
        P(("region", "col"), None),
        P(("region", "col"), None),
        P(("region", "col"), None, None),
        P(("region", "col"), None, None),
        P(),
        P(),
    )
    return jax.shard_map(
        local,
        mesh=mesh,
        in_specs=placed,
        out_specs=(P(("region", "col"), None, None), P(("region", "col"), None, None), P()),
        check_vma=False,
    )
```

```python
import jax
import jax.numpy as jnp
from jax import lax
from jax.sharding import PartitionSpec as P

ITERS = 2


def _pow2(n):
    return n >= 1 and (n & (n - 1)) == 0


def _exchange(x, axis, n, bit):
    return lax.ppermute(x, axis, [(i, i ^ (1 << bit)) for i in range(n)])


def _gather_order(n):
    bits = n.bit_length() - 1
    return list(range(1, bits)) + [0] if bits > 1 else list(range(bits))


def _slot(index, n):
    out = 0
    for m, bit in enumerate(_gather_order(n)):
        out = out + (((index >> bit) & 1) << m)
    return out


def _rounds(axis, sums, own=None, split=None):
    n = lax.axis_size(axis)
    if not _pow2(n) or n < 2:
        sums = [lax.psum(s, axis) for s in sums]
        full = None if split is None else lax.psum(split, axis)
        if own is not None:
            own = lax.all_gather(own, axis, axis=0, tiled=False)
        return full, sums, own
    shapes = [s.shape for s in sums]
    sizes = [s.size for s in sums]
    me = lax.axis_index(axis)
    order = _gather_order(n)
    bits = n.bit_length() - 1
    buf = None
    if own is not None:
        assert split is not None
        mine_slot = _slot(me, n)
        buf = jnp.zeros((n,) + own.shape, own.dtype)
        buf = lax.dynamic_update_index_in_dim(buf, own, mine_slot, 0)
    if split is not None:
        half = lax.rem(me, 2)
        halves = split.reshape((2, split.shape[0] // 2) + split.shape[1:])
        keep = lax.dynamic_index_in_dim(halves, half, 0, keepdims=False)
        give = lax.dynamic_index_in_dim(halves, 1 - half, 0, keepdims=False)
    steps = list(range(bits)) + ([0] if split is not None else [])
    m = 0
    for step, bit in enumerate(steps):
        last = split is not None and step == bits
        parts = []
        if split is not None:
            parts.append((give if step == 0 else keep).reshape(-1))
        if not last:
            parts += [s.reshape(-1) for s in sums]
        carry = buf is not None and m < bits and order[m] == bit and (step > 0 or bits == 1)
        if carry:
            used = sum(p.shape[0] for p in parts)
            if used % 1024:
                parts.append(jnp.zeros((-used % 1024,), jnp.float32))
            start = (mine_slot >> m) << m
            parts.append(lax.dynamic_slice_in_dim(buf, start, 1 << m, axis=0).reshape(-1))
        flat = jnp.concatenate(parts) if len(parts) > 1 else parts[0]
        got = _exchange(flat, axis, n, bit)
        off = 0
        if split is not None:
            piece = got[: keep.size].reshape(keep.shape)
            if last:
                other = piece
            else:
                keep = keep + piece
            off = keep.size
        if not last:
            new_sums = []
            for shape, size, s in zip(shapes, sizes, sums):
                new_sums.append(s + got[off : off + size].reshape(shape))
                off += size
            sums = new_sums
        if carry:
            off += -off % 1024
            theirs = ((mine_slot ^ (1 << m)) >> m) << m
            chunk = got[off:].reshape((1 << m,) + own.shape)
            buf = lax.dynamic_update_slice_in_dim(buf, chunk, theirs, axis=0)
            m += 1
    full = None
    if split is not None:
        both = jnp.concatenate([keep, other, keep], axis=0)
        full = lax.dynamic_slice_in_dim(both, half * keep.shape[0], 2 * keep.shape[0], axis=0)
    return full, sums, buf


def local(
    tiles,
    tile_rows,
    tile_cols,
    tile_count,
    rhs,
    base_cost,
    upper,
    primal,
    dual,
    price_levels,
    scenario_ids,
):
    hp = lax.Precision.HIGHEST
    ntiles = tiles.shape[0]
    row_blocks = rhs.shape[0]
    own_blocks = base_cost.shape[0]
    scenarios = primal.shape[1]
    lanes = primal.shape[2]
    ncol = lax.axis_size("col")
    region_blocks = own_blocks * ncol
    devices = lax.axis_size(("region", "col"))
    me = lax.axis_index("col")
    live = (jnp.arange(ntiles, dtype=jnp.int32) < tile_count[0]).astype(jnp.float32)
    choose = (
        scenario_ids[:, None] == jnp.arange(price_levels.shape[0], dtype=jnp.int32)[None, :]
    ).astype(jnp.float32)
    factor = jnp.dot(choose, price_levels, precision=hp)
    cost = base_cost[:, None, :] * factor[None, :, :]
    local_a = jnp.sum(jnp.sum(tiles * tiles, axis=(1, 2)) * live)
    local_c = jnp.sum(cost * cost, axis=(0, 2))
    local_b = jnp.sum(rhs * rhs)
    width = scenarios * lanes

    slot_cols = _slot(tile_cols // own_blocks, ncol) * own_blocks + tile_cols % own_blocks
    place = slot_cols * row_blocks + tile_rows
    place_live = (
        place[None, :] == jnp.arange(region_blocks * row_blocks, dtype=jnp.int32)[:, None]
    ).astype(jnp.float32) * live[None, :]

    def transposed_product(dual):
        return jnp.einsum("rsi,ricj->csj", dual, dense, precision=lax.Precision.HIGH)

    def product_of(point):
        return jnp.einsum("ricj,csj->rsi", dense, point, precision=lax.Precision.HIGH)

    norms = jnp.concatenate([local_a.reshape(1), local_c, local_b.reshape(1)])
    n_region = lax.axis_size("region")
    by_row = place_live.reshape(region_blocks, row_blocks, ntiles).transpose(1, 0, 2)

    def build(r, by_row):
        return jnp.dot(by_row[r], tiles.reshape(ntiles, -1), precision=hp)

    first = build(0, by_row)
    if _pow2(n_region) and n_region >= 2:
        norms = norms + _exchange(norms, "region", n_region, 0)
        norms, by_row = lax.optimization_barrier((norms, by_row))
        for bit in range(1, n_region.bit_length() - 1):
            norms = norms + _exchange(norms, "region", n_region, bit)
    else:
        norms = lax.psum(norms, "region")
    dense = jnp.stack([first] + [build(r, by_row) for r in range(1, row_blocks)])
    dense = dense.reshape(row_blocks, region_blocks, tiles.shape[1], tiles.shape[2])
    dense = dense.transpose(0, 2, 1, 3)
    own_rows = own_blocks * (scenarios + 2)
    own = jnp.concatenate(
        [
            primal.reshape(own_blocks * scenarios, lanes),
            base_cost,
            upper,
            jnp.zeros((-own_rows % 8, lanes), jnp.float32),
        ],
        axis=0,
    )
    partial_value = transposed_product(dual)
    grad, (norms,), gathered = _rounds("col", [norms], own, split=partial_value)
    sq_a, sq_c, sq_b = norms[0], norms[1 : scenarios + 1], norms[scenarios + 1]
    primal_reg = gathered[:, : own_blocks * scenarios].reshape(region_blocks, scenarios, lanes)
    base_reg = gathered[:, own_blocks * scenarios : own_blocks * (scenarios + 1)]
    upper_reg = gathered[:, own_blocks * (scenarios + 1) : own_rows]
    cost_reg = base_reg.reshape(region_blocks, lanes)[:, None, :] * factor[None, :, :]
    upper_reg = upper_reg.reshape(region_blocks, lanes)[:, None, :]
    eta = 0.5 / jnp.sqrt(sq_a / (lanes * row_blocks * devices))
    weight = jnp.sqrt(sq_c) / jnp.sqrt(sq_b)
    for step in range(ITERS):
        if step > 0:
            _, (step_x, part_y), _ = _rounds("region", [local_x, local_y])
            partial_value = transposed_product(dual)
            grad, (step_y,), _ = _rounds("col", [part_y], split=partial_value)
            weight = jnp.sqrt(weight * jnp.sqrt((step_x + 1e-06) / (step_y + 1e-06)))
        tau = (eta / weight)[None, :, None]
        sigma = (eta * weight)[None, :, None]
        new_primal = jnp.clip(primal_reg - tau * (cost_reg - grad), 0.0, upper_reg)
        point = 2.0 * new_primal - primal_reg
        product = product_of(point)
        new_dual = jnp.maximum(dual + sigma * (rhs[:, None, :] - product), 0.0)
        local_x = jnp.sum((new_primal - primal_reg) ** 2, axis=(0, 2))
        local_y = jnp.sum((new_dual - dual) ** 2, axis=(0, 2))
        primal_reg, dual = (new_primal, new_dual)
    _, (step_x, part_y), _ = _rounds("region", [local_x, local_y])
    _, (step_y,), _ = _rounds("col", [part_y])
    weight = jnp.sqrt(weight * jnp.sqrt((step_x + 1e-06) / (step_y + 1e-06)))
    primal_out = lax.dynamic_slice_in_dim(
        primal_reg, _slot(me, ncol) * own_blocks, own_blocks, axis=0
    )
    return (primal_out, dual, weight)


def solution(mesh):
    placed = (
        P(("region", "col"), None, None),
        P(("region", "col")),
        P(("region", "col")),
        P(("region", "col")),
        P(("region", "col"), None),
        P(("region", "col"), None),
        P(("region", "col"), None),
        P(("region", "col"), None, None),
        P(("region", "col"), None, None),
        P(),
        P(),
    )
    return jax.shard_map(
        local,
        mesh=mesh,
        in_specs=placed,
        out_specs=(P(("region", "col"), None, None), P(("region", "col"), None, None), P()),
        check_vma=False,
    )
```

```python
import jax
import jax.numpy as jnp
from jax import lax
from jax.sharding import PartitionSpec as P

ITERS = 2


def _pow2(n):
    return n >= 1 and (n & (n - 1)) == 0


def _exchange(x, axis, n, bit):
    return lax.ppermute(x, axis, [(i, i ^ (1 << bit)) for i in range(n)])


def _gather_order(n):
    bits = n.bit_length() - 1
    return list(range(1, bits)) + [0] if bits > 1 else list(range(bits))


def _slot(index, n):
    out = 0
    for m, bit in enumerate(_gather_order(n)):
        out = out + (((index >> bit) & 1) << m)
    return out


def _rounds(axis, sums, own=None, split=None):
    n = lax.axis_size(axis)
    if not _pow2(n) or n < 2:
        sums = [lax.psum(s, axis) for s in sums]
        full = None if split is None else lax.psum(split, axis)
        if own is not None:
            own = lax.all_gather(own, axis, axis=0, tiled=False)
        return full, sums, own
    shapes = [s.shape for s in sums]
    sizes = [s.size for s in sums]
    me = lax.axis_index(axis)
    order = _gather_order(n)
    bits = n.bit_length() - 1
    buf = None
    if own is not None:
        assert split is not None
        mine_slot = _slot(me, n)
        buf = jnp.zeros((n,) + own.shape, own.dtype)
        buf = lax.dynamic_update_index_in_dim(buf, own, mine_slot, 0)
    if split is not None:
        half = lax.rem(me, 2)
        halves = split.reshape((2, split.shape[0] // 2) + split.shape[1:])
        keep = lax.dynamic_index_in_dim(halves, half, 0, keepdims=False)
        give = lax.dynamic_index_in_dim(halves, 1 - half, 0, keepdims=False)
    steps = list(range(bits)) + ([0] if split is not None else [])
    m = 0
    for step, bit in enumerate(steps):
        last = split is not None and step == bits
        parts = []
        if split is not None:
            parts.append((give if step == 0 else keep).reshape(-1))
        if not last:
            parts += [s.reshape(-1) for s in sums]
        carry = buf is not None and m < bits and order[m] == bit and (step > 0 or bits == 1)
        if carry:
            used = sum(p.shape[0] for p in parts)
            if used % 1024:
                parts.append(jnp.zeros((-used % 1024,), jnp.float32))
            start = (mine_slot >> m) << m
            parts.append(lax.dynamic_slice_in_dim(buf, start, 1 << m, axis=0).reshape(-1))
        flat = jnp.concatenate(parts) if len(parts) > 1 else parts[0]
        got = _exchange(flat, axis, n, bit)
        off = 0
        if split is not None:
            piece = got[: keep.size].reshape(keep.shape)
            if last:
                other = piece
            else:
                keep = keep + piece
            off = keep.size
        if not last:
            new_sums = []
            for shape, size, s in zip(shapes, sizes, sums):
                new_sums.append(s + got[off : off + size].reshape(shape))
                off += size
            sums = new_sums
        if carry:
            off += -off % 1024
            theirs = ((mine_slot ^ (1 << m)) >> m) << m
            chunk = got[off:].reshape((1 << m,) + own.shape)
            buf = lax.dynamic_update_slice_in_dim(buf, chunk, theirs, axis=0)
            m += 1
    full = None
    if split is not None:
        both = jnp.concatenate([keep, other, keep], axis=0)
        full = lax.dynamic_slice_in_dim(both, half * keep.shape[0], 2 * keep.shape[0], axis=0)
    return full, sums, buf


def local(
    tiles,
    tile_rows,
    tile_cols,
    tile_count,
    rhs,
    base_cost,
    upper,
    primal,
    dual,
    price_levels,
    scenario_ids,
):
    hp = lax.Precision.HIGHEST
    ntiles = tiles.shape[0]
    row_blocks = rhs.shape[0]
    own_blocks = base_cost.shape[0]
    scenarios = primal.shape[1]
    lanes = primal.shape[2]
    ncol = lax.axis_size("col")
    region_blocks = own_blocks * ncol
    devices = lax.axis_size(("region", "col"))
    me = lax.axis_index("col")
    live = (jnp.arange(ntiles, dtype=jnp.int32) < tile_count[0]).astype(jnp.float32)
    choose = (
        scenario_ids[:, None] == jnp.arange(price_levels.shape[0], dtype=jnp.int32)[None, :]
    ).astype(jnp.float32)
    factor = jnp.dot(choose, price_levels, precision=hp)
    cost = base_cost[:, None, :] * factor[None, :, :]
    local_a = jnp.sum(tiles * tiles * live[:, None, None], axis=(0, 1))
    local_c = jnp.sum(cost * cost, axis=(0, 2))
    local_b = jnp.sum(rhs * rhs, axis=0)
    width = scenarios * lanes

    slot_cols = _slot(tile_cols // own_blocks, ncol) * own_blocks + tile_cols % own_blocks
    place = slot_cols * row_blocks + tile_rows
    place_live = (
        place[None, :] == jnp.arange(region_blocks * row_blocks, dtype=jnp.int32)[:, None]
    ).astype(jnp.float32) * live[None, :]
    dense = jnp.dot(place_live, tiles.reshape(ntiles, -1), precision=hp)
    dense = dense.reshape(region_blocks, row_blocks, tiles.shape[1], tiles.shape[2])
    dense = dense.transpose(1, 2, 0, 3)

    def transposed_product(dual):
        return jnp.einsum("rsi,ricj->csj", dual, dense, precision=lax.Precision.HIGH)

    def product_of(point):
        return jnp.einsum("ricj,csj->rsi", dense, point, precision=lax.Precision.HIGH)

    norms = jnp.concatenate([local_a, local_b, local_c])
    _, (norms,), _ = _rounds("region", [norms])
    own_rows = own_blocks * (scenarios + 2)
    own = jnp.concatenate(
        [
            primal.reshape(own_blocks * scenarios, lanes),
            base_cost,
            upper,
            jnp.zeros((-own_rows % 8, lanes), jnp.float32),
        ],
        axis=0,
    )
    partial_value = transposed_product(dual)
    grad, (norms,), gathered = _rounds("col", [norms], own, split=partial_value)
    sq_a = jnp.sum(norms[:lanes])
    sq_b = jnp.sum(norms[lanes : 2 * lanes])
    sq_c = norms[2 * lanes :]
    primal_reg = gathered[:, : own_blocks * scenarios].reshape(region_blocks, scenarios, lanes)
    base_reg = gathered[:, own_blocks * scenarios : own_blocks * (scenarios + 1)]
    upper_reg = gathered[:, own_blocks * (scenarios + 1) : own_rows]
    cost_reg = base_reg.reshape(region_blocks, lanes)[:, None, :] * factor[None, :, :]
    upper_reg = upper_reg.reshape(region_blocks, lanes)[:, None, :]
    eta = 0.5 / jnp.sqrt(sq_a / (lanes * row_blocks * devices))
    weight = jnp.sqrt(sq_c) / jnp.sqrt(sq_b)
    for step in range(ITERS):
        if step > 0:
            _, (step_x, part_y), _ = _rounds("region", [local_x, local_y])
            partial_value = transposed_product(dual)
            grad, (step_y,), _ = _rounds("col", [part_y], split=partial_value)
            weight = jnp.sqrt(weight * jnp.sqrt((step_x + 1e-06) / (step_y + 1e-06)))
        tau = (eta / weight)[None, :, None]
        sigma = (eta * weight)[None, :, None]
        new_primal = jnp.clip(primal_reg - tau * (cost_reg - grad), 0.0, upper_reg)
        point = 2.0 * new_primal - primal_reg
        product = product_of(point)
        new_dual = jnp.maximum(dual + sigma * (rhs[:, None, :] - product), 0.0)
        local_x = jnp.sum((new_primal - primal_reg) ** 2, axis=(0, 2))
        local_y = jnp.sum((new_dual - dual) ** 2, axis=(0, 2))
        primal_reg, dual = (new_primal, new_dual)
    _, (step_x, part_y), _ = _rounds("region", [local_x, local_y])
    _, (step_y,), _ = _rounds("col", [part_y])
    weight = jnp.sqrt(weight * jnp.sqrt((step_x + 1e-06) / (step_y + 1e-06)))
    primal_out = lax.dynamic_slice_in_dim(
        primal_reg, _slot(me, ncol) * own_blocks, own_blocks, axis=0
    )
    return (primal_out, dual, weight)


def solution(mesh):
    placed = (
        P(("region", "col"), None, None),
        P(("region", "col")),
        P(("region", "col")),
        P(("region", "col")),
        P(("region", "col"), None),
        P(("region", "col"), None),
        P(("region", "col"), None),
        P(("region", "col"), None, None),
        P(("region", "col"), None, None),
        P(),
        P(),
    )
    return jax.shard_map(
        local,
        mesh=mesh,
        in_specs=placed,
        out_specs=(P(("region", "col"), None, None), P(("region", "col"), None, None), P()),
        check_vma=False,
    )
```

```python
import jax
import jax.numpy as jnp
from jax import lax
from jax.sharding import PartitionSpec as P

ITERS = 2


def _pow2(n):
    return n >= 1 and (n & (n - 1)) == 0


def _exchange(x, axis, n, bit):
    return lax.ppermute(x, axis, [(i, i ^ (1 << bit)) for i in range(n)])


def _gather_order(n):
    bits = n.bit_length() - 1
    return list(range(1, bits)) + [0] if bits > 1 else list(range(bits))


def _slot(index, n):
    out = 0
    for m, bit in enumerate(_gather_order(n)):
        out = out + (((index >> bit) & 1) << m)
    return out


def _rounds(axis, sums, own=None, split=None):
    n = lax.axis_size(axis)
    if not _pow2(n) or n < 2:
        sums = [lax.psum(s, axis) for s in sums]
        full = None if split is None else lax.psum(split, axis)
        if own is not None:
            own = lax.all_gather(own, axis, axis=0, tiled=False)
        return full, sums, own
    shapes = [s.shape for s in sums]
    sizes = [s.size for s in sums]
    me = lax.axis_index(axis)
    order = _gather_order(n)
    bits = n.bit_length() - 1
    buf = None
    if own is not None:
        assert split is not None
        mine_slot = _slot(me, n)
        buf = jnp.zeros((n,) + own.shape, own.dtype)
        buf = lax.dynamic_update_index_in_dim(buf, own, mine_slot, 0)
    if split is not None:
        half = lax.rem(me, 2)
        halves = split.reshape((2, split.shape[0] // 2) + split.shape[1:])
        keep = lax.dynamic_index_in_dim(halves, half, 0, keepdims=False)
        give = lax.dynamic_index_in_dim(halves, 1 - half, 0, keepdims=False)
    steps = list(range(bits)) + ([0] if split is not None else [])
    m = 0
    for step, bit in enumerate(steps):
        last = split is not None and step == bits
        parts = []
        if split is not None:
            parts.append((give if step == 0 else keep).reshape(-1))
        if not last:
            parts += [s.reshape(-1) for s in sums]
        carry = buf is not None and m < bits and order[m] == bit and (step > 0 or bits == 1)
        if carry:
            used = sum(p.shape[0] for p in parts)
            if used % 1024:
                parts.append(jnp.zeros((-used % 1024,), jnp.float32))
            start = (mine_slot >> m) << m
            parts.append(lax.dynamic_slice_in_dim(buf, start, 1 << m, axis=0).reshape(-1))
        flat = jnp.concatenate(parts) if len(parts) > 1 else parts[0]
        got = _exchange(flat, axis, n, bit)
        off = 0
        if split is not None:
            piece = got[: keep.size].reshape(keep.shape)
            if last:
                other = piece
            else:
                keep = keep + piece
            off = keep.size
        if not last:
            new_sums = []
            for shape, size, s in zip(shapes, sizes, sums):
                new_sums.append(s + got[off : off + size].reshape(shape))
                off += size
            sums = new_sums
        if carry:
            off += -off % 1024
            theirs = ((mine_slot ^ (1 << m)) >> m) << m
            chunk = got[off:].reshape((1 << m,) + own.shape)
            buf = lax.dynamic_update_slice_in_dim(buf, chunk, theirs, axis=0)
            m += 1
    full = None
    if split is not None:
        both = jnp.concatenate([keep, other, keep], axis=0)
        full = lax.dynamic_slice_in_dim(both, half * keep.shape[0], 2 * keep.shape[0], axis=0)
    return full, sums, buf


def local(
    tiles,
    tile_rows,
    tile_cols,
    tile_count,
    rhs,
    base_cost,
    upper,
    primal,
    dual,
    price_levels,
    scenario_ids,
):
    hp = lax.Precision.HIGHEST
    ntiles = tiles.shape[0]
    row_blocks = rhs.shape[0]
    own_blocks = base_cost.shape[0]
    scenarios = primal.shape[1]
    lanes = primal.shape[2]
    ncol = lax.axis_size("col")
    region_blocks = own_blocks * ncol
    devices = lax.axis_size(("region", "col"))
    me = lax.axis_index("col")
    live = (jnp.arange(ntiles, dtype=jnp.int32) < tile_count[0]).astype(jnp.float32)
    choose = (
        scenario_ids[:, None] == jnp.arange(price_levels.shape[0], dtype=jnp.int32)[None, :]
    ).astype(jnp.float32)
    factor = jnp.dot(choose, price_levels, precision=hp)
    cost = base_cost[:, None, :] * factor[None, :, :]
    local_a = jnp.sum(tiles * tiles * live[:, None, None], axis=(0, 1))
    local_c = jnp.sum(cost * cost, axis=(0, 2))
    local_b = jnp.sum(rhs * rhs, axis=0)
    width = scenarios * lanes

    slot_cols = _slot(tile_cols // own_blocks, ncol) * own_blocks + tile_cols % own_blocks
    place = slot_cols * row_blocks + tile_rows
    place_live = (
        place[None, :] == jnp.arange(region_blocks * row_blocks, dtype=jnp.int32)[:, None]
    ).astype(jnp.float32) * live[None, :]
    dense = jnp.dot(place_live, tiles.reshape(ntiles, -1), precision=hp)
    dense = dense.reshape(region_blocks, row_blocks, tiles.shape[1], tiles.shape[2])
    dense = dense.transpose(1, 2, 0, 3)

    def transposed_product(dual):
        return jnp.einsum("rsi,ricj->csj", dual, dense, precision=lax.Precision.HIGH)

    def product_of(point):
        return jnp.einsum("ricj,csj->rsi", dense, point, precision=lax.Precision.HIGH)

    norms = jnp.concatenate([local_a, local_b, local_c])
    _, (norms,), _ = _rounds("region", [norms])
    own_rows = own_blocks * (scenarios + 2)
    own = jnp.concatenate(
        [
            primal.reshape(own_blocks * scenarios, lanes),
            base_cost,
            upper,
            jnp.zeros((-own_rows % 8, lanes), jnp.float32),
        ],
        axis=0,
    )
    partial_value = transposed_product(dual)
    grad, (norms,), gathered = _rounds("col", [norms], own, split=partial_value)
    sq_a = jnp.sum(jnp.broadcast_to(norms[:lanes], (scenarios, lanes)), axis=1)
    sq_b = jnp.sum(jnp.broadcast_to(norms[lanes : 2 * lanes], (scenarios, lanes)), axis=1)
    sq_c = norms[2 * lanes :]
    primal_reg = gathered[:, : own_blocks * scenarios].reshape(region_blocks, scenarios, lanes)
    base_reg = gathered[:, own_blocks * scenarios : own_blocks * (scenarios + 1)]
    upper_reg = gathered[:, own_blocks * (scenarios + 1) : own_rows]
    cost_reg = base_reg.reshape(region_blocks, lanes)[:, None, :] * factor[None, :, :]
    upper_reg = upper_reg.reshape(region_blocks, lanes)[:, None, :]
    eta = 0.5 / jnp.sqrt(sq_a / (lanes * row_blocks * devices))
    weight = jnp.sqrt(sq_c) / jnp.sqrt(sq_b)
    for step in range(ITERS):
        if step > 0:
            _, (step_x, part_y), _ = _rounds("region", [local_x, local_y])
            partial_value = transposed_product(dual)
            grad, (step_y,), _ = _rounds("col", [part_y], split=partial_value)
            weight = jnp.sqrt(weight * jnp.sqrt((step_x + 1e-06) / (step_y + 1e-06)))
        tau = (eta / weight)[None, :, None]
        sigma = (eta * weight)[None, :, None]
        new_primal = jnp.clip(primal_reg - tau * (cost_reg - grad), 0.0, upper_reg)
        point = 2.0 * new_primal - primal_reg
        product = product_of(point)
        new_dual = jnp.maximum(dual + sigma * (rhs[:, None, :] - product), 0.0)
        local_x = jnp.sum((new_primal - primal_reg) ** 2, axis=(0, 2))
        local_y = jnp.sum((new_dual - dual) ** 2, axis=(0, 2))
        primal_reg, dual = (new_primal, new_dual)
    _, (step_x, part_y), _ = _rounds("region", [local_x, local_y])
    _, (step_y,), _ = _rounds("col", [part_y])
    weight = jnp.sqrt(weight * jnp.sqrt((step_x + 1e-06) / (step_y + 1e-06)))
    primal_out = lax.dynamic_slice_in_dim(
        primal_reg, _slot(me, ncol) * own_blocks, own_blocks, axis=0
    )
    return (primal_out, dual, weight)


def solution(mesh):
    placed = (
        P(("region", "col"), None, None),
        P(("region", "col")),
        P(("region", "col")),
        P(("region", "col")),
        P(("region", "col"), None),
        P(("region", "col"), None),
        P(("region", "col"), None),
        P(("region", "col"), None, None),
        P(("region", "col"), None, None),
        P(),
        P(),
    )
    return jax.shard_map(
        local,
        mesh=mesh,
        in_specs=placed,
        out_specs=(P(("region", "col"), None, None), P(("region", "col"), None, None), P()),
        check_vma=False,
    )
```

```python
import jax
import jax.numpy as jnp
from jax import lax
from jax.sharding import PartitionSpec as P

ITERS = 2


def _pow2(n):
    return n >= 1 and (n & (n - 1)) == 0


def _exchange(x, axis, n, bit):
    return lax.ppermute(x, axis, [(i, i ^ (1 << bit)) for i in range(n)])


def _gather_order(n):
    bits = n.bit_length() - 1
    return list(range(1, bits)) + [0] if bits > 1 else list(range(bits))


def _slot(index, n):
    out = 0
    for m, bit in enumerate(_gather_order(n)):
        out = out + (((index >> bit) & 1) << m)
    return out


def _rounds(axis, sums, own=None, split=None):
    n = lax.axis_size(axis)
    if not _pow2(n) or n < 2:
        sums = [lax.psum(s, axis) for s in sums]
        full = None if split is None else lax.psum(split, axis)
        if own is not None:
            own = lax.all_gather(own, axis, axis=0, tiled=False)
        return full, sums, own
    shapes = [s.shape for s in sums]
    sizes = [s.size for s in sums]
    me = lax.axis_index(axis)
    order = _gather_order(n)
    bits = n.bit_length() - 1
    buf = None
    if own is not None:
        assert split is not None
        mine_slot = _slot(me, n)
        buf = jnp.zeros((n,) + own.shape, own.dtype)
        buf = lax.dynamic_update_index_in_dim(buf, own, mine_slot, 0)
    if split is not None:
        half = lax.rem(me, 2)
        halves = split.reshape((2, split.shape[0] // 2) + split.shape[1:])
        keep = lax.dynamic_index_in_dim(halves, half, 0, keepdims=False)
        give = lax.dynamic_index_in_dim(halves, 1 - half, 0, keepdims=False)
    steps = list(range(bits)) + ([0] if split is not None else [])
    m = 0
    for step, bit in enumerate(steps):
        last = split is not None and step == bits
        parts = []
        if split is not None:
            parts.append((give if step == 0 else keep).reshape(-1))
        if not last:
            parts += [s.reshape(-1) for s in sums]
        carry = buf is not None and m < bits and order[m] == bit and (step > 0 or bits == 1)
        if carry:
            used = sum(p.shape[0] for p in parts)
            if used % 1024:
                parts.append(jnp.zeros((-used % 1024,), jnp.float32))
            start = (mine_slot >> m) << m
            parts.append(lax.dynamic_slice_in_dim(buf, start, 1 << m, axis=0).reshape(-1))
        flat = jnp.concatenate(parts) if len(parts) > 1 else parts[0]
        got = _exchange(flat, axis, n, bit)
        off = 0
        if split is not None:
            piece = got[: keep.size].reshape(keep.shape)
            if last:
                other = piece
            else:
                keep = keep + piece
            off = keep.size
        if not last:
            new_sums = []
            for shape, size, s in zip(shapes, sizes, sums):
                new_sums.append(s + got[off : off + size].reshape(shape))
                off += size
            sums = new_sums
        if carry:
            off += -off % 1024
            theirs = ((mine_slot ^ (1 << m)) >> m) << m
            chunk = got[off:].reshape((1 << m,) + own.shape)
            buf = lax.dynamic_update_slice_in_dim(buf, chunk, theirs, axis=0)
            m += 1
    full = None
    if split is not None:
        both = jnp.concatenate([keep, other, keep], axis=0)
        full = lax.dynamic_slice_in_dim(both, half * keep.shape[0], 2 * keep.shape[0], axis=0)
    return full, sums, buf


def local(
    tiles,
    tile_rows,
    tile_cols,
    tile_count,
    rhs,
    base_cost,
    upper,
    primal,
    dual,
    price_levels,
    scenario_ids,
):
    hp = lax.Precision.HIGHEST
    ntiles = tiles.shape[0]
    row_blocks = rhs.shape[0]
    own_blocks = base_cost.shape[0]
    scenarios = primal.shape[1]
    lanes = primal.shape[2]
    ncol = lax.axis_size("col")
    region_blocks = own_blocks * ncol
    devices = lax.axis_size(("region", "col"))
    me = lax.axis_index("col")
    live = (jnp.arange(ntiles, dtype=jnp.int32) < tile_count[0]).astype(jnp.float32)
    choose = (
        scenario_ids[:, None] == jnp.arange(price_levels.shape[0], dtype=jnp.int32)[None, :]
    ).astype(jnp.float32)
    factor = jnp.dot(choose, price_levels, precision=hp)
    cost = base_cost[:, None, :] * factor[None, :, :]
    local_a = jnp.sum(tiles * tiles * live[:, None, None], axis=(0, 1))
    local_c = jnp.sum(cost * cost, axis=(0, 2))
    local_b = jnp.sum(rhs * rhs, axis=0)
    width = scenarios * lanes

    slot_cols = _slot(tile_cols // own_blocks, ncol) * own_blocks + tile_cols % own_blocks
    place = slot_cols * row_blocks + tile_rows
    place_live = (
        place[None, :] == jnp.arange(region_blocks * row_blocks, dtype=jnp.int32)[:, None]
    ).astype(jnp.float32) * live[None, :]
    dense = jnp.dot(place_live, tiles.reshape(ntiles, -1), precision=hp)
    dense = dense.reshape(region_blocks, row_blocks, tiles.shape[1], tiles.shape[2])
    dense = dense.transpose(1, 2, 0, 3)

    def transposed_product(dual):
        return jnp.einsum("rsi,ricj->csj", dual, dense, precision=lax.Precision.HIGH)

    def product_of(point):
        return jnp.einsum("ricj,csj->rsi", dense, point, precision=lax.Precision.HIGH)

    norms = jnp.concatenate([local_a, local_b, local_c])
    n_region = lax.axis_size("region")
    if _pow2(n_region) and n_region >= 2:
        norms = norms + _exchange(norms, "region", n_region, 0)
        norms, dense = lax.optimization_barrier((norms, dense))
        for bit in range(1, n_region.bit_length() - 1):
            norms = norms + _exchange(norms, "region", n_region, bit)
    else:
        norms = lax.psum(norms, "region")
    own_rows = own_blocks * (scenarios + 2)
    own = jnp.concatenate(
        [
            primal.reshape(own_blocks * scenarios, lanes),
            base_cost,
            upper,
            jnp.zeros((-own_rows % 8, lanes), jnp.float32),
        ],
        axis=0,
    )
    partial_value = transposed_product(dual)
    grad, (norms,), gathered = _rounds("col", [norms], own, split=partial_value)
    sq_a = jnp.sum(norms[:lanes])
    sq_b = jnp.sum(norms[lanes : 2 * lanes])
    sq_c = norms[2 * lanes :]
    primal_reg = gathered[:, : own_blocks * scenarios].reshape(region_blocks, scenarios, lanes)
    base_reg = gathered[:, own_blocks * scenarios : own_blocks * (scenarios + 1)]
    upper_reg = gathered[:, own_blocks * (scenarios + 1) : own_rows]
    cost_reg = base_reg.reshape(region_blocks, lanes)[:, None, :] * factor[None, :, :]
    upper_reg = upper_reg.reshape(region_blocks, lanes)[:, None, :]
    eta = 0.5 / jnp.sqrt(sq_a / (lanes * row_blocks * devices))
    weight = jnp.sqrt(sq_c) / jnp.sqrt(sq_b)
    for step in range(ITERS):
        if step > 0:
            _, (step_x, part_y), _ = _rounds("region", [local_x, local_y])
            partial_value = transposed_product(dual)
            grad, (step_y,), _ = _rounds("col", [part_y], split=partial_value)
            weight = jnp.sqrt(weight * jnp.sqrt((step_x + 1e-06) / (step_y + 1e-06)))
        tau = (eta / weight)[None, :, None]
        sigma = (eta * weight)[None, :, None]
        new_primal = jnp.clip(primal_reg - tau * (cost_reg - grad), 0.0, upper_reg)
        point = 2.0 * new_primal - primal_reg
        product = product_of(point)
        new_dual = jnp.maximum(dual + sigma * (rhs[:, None, :] - product), 0.0)
        local_x = jnp.sum((new_primal - primal_reg) ** 2, axis=(0, 2))
        local_y = jnp.sum((new_dual - dual) ** 2, axis=(0, 2))
        primal_reg, dual = (new_primal, new_dual)
    _, (step_x, part_y), _ = _rounds("region", [local_x, local_y])
    _, (step_y,), _ = _rounds("col", [part_y])
    weight = jnp.sqrt(weight * jnp.sqrt((step_x + 1e-06) / (step_y + 1e-06)))
    primal_out = lax.dynamic_slice_in_dim(
        primal_reg, _slot(me, ncol) * own_blocks, own_blocks, axis=0
    )
    return (primal_out, dual, weight)


def solution(mesh):
    placed = (
        P(("region", "col"), None, None),
        P(("region", "col")),
        P(("region", "col")),
        P(("region", "col")),
        P(("region", "col"), None),
        P(("region", "col"), None),
        P(("region", "col"), None),
        P(("region", "col"), None, None),
        P(("region", "col"), None, None),
        P(),
        P(),
    )
    return jax.shard_map(
        local,
        mesh=mesh,
        in_specs=placed,
        out_specs=(P(("region", "col"), None, None), P(("region", "col"), None, None), P()),
        check_vma=False,
    )
```

```python
import jax
import jax.numpy as jnp
from jax import lax
from jax.sharding import PartitionSpec as P

ITERS = 2


def _pow2(n):
    return n >= 1 and (n & (n - 1)) == 0


def _exchange(x, axis, n, bit):
    return lax.ppermute(x, axis, [(i, i ^ (1 << bit)) for i in range(n)])


def _gather_order(n):
    bits = n.bit_length() - 1
    return list(range(1, bits)) + [0] if bits > 1 else list(range(bits))


def _slot(index, n):
    out = 0
    for m, bit in enumerate(_gather_order(n)):
        out = out + (((index >> bit) & 1) << m)
    return out


def _rounds(axis, sums, own=None, split=None):
    n = lax.axis_size(axis)
    if not _pow2(n) or n < 2:
        sums = [lax.psum(s, axis) for s in sums]
        full = None if split is None else lax.psum(split, axis)
        if own is not None:
            own = lax.all_gather(own, axis, axis=0, tiled=False)
        return full, sums, own
    shapes = [s.shape for s in sums]
    sizes = [s.size for s in sums]
    me = lax.axis_index(axis)
    order = _gather_order(n)
    bits = n.bit_length() - 1
    buf = None
    if own is not None:
        assert split is not None
        mine_slot = _slot(me, n)
        buf = jnp.zeros((n,) + own.shape, own.dtype)
        buf = lax.dynamic_update_index_in_dim(buf, own, mine_slot, 0)
    if split is not None:
        half = lax.rem(me, 2)
        halves = split.reshape((2, split.shape[0] // 2) + split.shape[1:])
        keep = lax.dynamic_index_in_dim(halves, half, 0, keepdims=False)
        give = lax.dynamic_index_in_dim(halves, 1 - half, 0, keepdims=False)
    steps = list(range(bits)) + ([0] if split is not None else [])
    m = 0
    for step, bit in enumerate(steps):
        last = split is not None and step == bits
        parts = []
        if split is not None:
            parts.append((give if step == 0 else keep).reshape(-1))
        if not last:
            parts += [s.reshape(-1) for s in sums]
        carry = buf is not None and m < bits and order[m] == bit and (step > 0 or bits == 1)
        if carry:
            used = sum(p.shape[0] for p in parts)
            if used % 1024:
                parts.append(jnp.zeros((-used % 1024,), jnp.float32))
            start = (mine_slot >> m) << m
            parts.append(lax.dynamic_slice_in_dim(buf, start, 1 << m, axis=0).reshape(-1))
        flat = jnp.concatenate(parts) if len(parts) > 1 else parts[0]
        got = _exchange(flat, axis, n, bit)
        off = 0
        if split is not None:
            piece = got[: keep.size].reshape(keep.shape)
            if last:
                other = piece
            else:
                keep = keep + piece
            off = keep.size
        if not last:
            new_sums = []
            for shape, size, s in zip(shapes, sizes, sums):
                new_sums.append(s + got[off : off + size].reshape(shape))
                off += size
            sums = new_sums
        if carry:
            off += -off % 1024
            theirs = ((mine_slot ^ (1 << m)) >> m) << m
            chunk = got[off:].reshape((1 << m,) + own.shape)
            buf = lax.dynamic_update_slice_in_dim(buf, chunk, theirs, axis=0)
            m += 1
    full = None
    if split is not None:
        both = jnp.concatenate([keep, other, keep], axis=0)
        full = lax.dynamic_slice_in_dim(both, half * keep.shape[0], 2 * keep.shape[0], axis=0)
    return full, sums, buf


def local(
    tiles,
    tile_rows,
    tile_cols,
    tile_count,
    rhs,
    base_cost,
    upper,
    primal,
    dual,
    price_levels,
    scenario_ids,
):
    hp = lax.Precision.HIGHEST
    ntiles = tiles.shape[0]
    row_blocks = rhs.shape[0]
    own_blocks = base_cost.shape[0]
    scenarios = primal.shape[1]
    lanes = primal.shape[2]
    ncol = lax.axis_size("col")
    region_blocks = own_blocks * ncol
    devices = lax.axis_size(("region", "col"))
    me = lax.axis_index("col")
    live = (jnp.arange(ntiles, dtype=jnp.int32) < tile_count[0]).astype(jnp.float32)
    choose = (
        scenario_ids[:, None] == jnp.arange(price_levels.shape[0], dtype=jnp.int32)[None, :]
    ).astype(jnp.float32)
    factor = jnp.dot(choose, price_levels, precision=hp)
    cost = base_cost[:, None, :] * factor[None, :, :]
    local_a = jnp.sum(tiles * tiles * live[:, None, None], axis=(0, 1))
    local_c = jnp.sum(cost * cost, axis=(0, 2))
    local_b = jnp.sum(rhs * rhs, axis=0)
    width = scenarios * lanes

    slot_cols = _slot(tile_cols // own_blocks, ncol) * own_blocks + tile_cols % own_blocks
    place = slot_cols * row_blocks + tile_rows
    place_live = (
        place[None, :] == jnp.arange(region_blocks * row_blocks, dtype=jnp.int32)[:, None]
    ).astype(jnp.float32) * live[None, :]
    dense = jnp.dot(place_live, tiles.reshape(ntiles, -1), precision=hp)
    dense = dense.reshape(region_blocks, row_blocks, tiles.shape[1], tiles.shape[2])
    dense = dense.transpose(1, 2, 0, 3)

    def transposed_product(dual):
        return jnp.einsum("rsi,ricj->csj", dual, dense, precision=lax.Precision.HIGH)

    def product_of(point):
        return jnp.einsum("ricj,csj->rsi", dense, point, precision=lax.Precision.HIGH)

    norms = jnp.concatenate([local_a, local_b, local_c])
    n_region = lax.axis_size("region")
    if _pow2(n_region) and n_region >= 2:
        norms = norms + _exchange(norms, "region", n_region, 0)
        norms, dense = lax.optimization_barrier((norms, dense))
        for bit in range(1, n_region.bit_length() - 1):
            norms = norms + _exchange(norms, "region", n_region, bit)
    else:
        norms = lax.psum(norms, "region")
    own_rows = own_blocks * (scenarios + 2)
    own = jnp.concatenate(
        [
            primal.reshape(own_blocks * scenarios, lanes),
            base_cost,
            upper,
            jnp.zeros((-own_rows % 8, lanes), jnp.float32),
        ],
        axis=0,
    )
    partial_value = transposed_product(dual)
    grad, (norms,), gathered = _rounds("col", [norms], own, split=partial_value)
    norms, grad = lax.optimization_barrier((norms, grad))
    sq_a = jnp.sum(norms[:lanes])
    sq_b = jnp.sum(norms[lanes : 2 * lanes])
    sq_c = norms[2 * lanes :]
    primal_reg = gathered[:, : own_blocks * scenarios].reshape(region_blocks, scenarios, lanes)
    base_reg = gathered[:, own_blocks * scenarios : own_blocks * (scenarios + 1)]
    upper_reg = gathered[:, own_blocks * (scenarios + 1) : own_rows]
    cost_reg = base_reg.reshape(region_blocks, lanes)[:, None, :] * factor[None, :, :]
    upper_reg = upper_reg.reshape(region_blocks, lanes)[:, None, :]
    eta = 0.5 / jnp.sqrt(sq_a / (lanes * row_blocks * devices))
    weight = jnp.sqrt(sq_c) / jnp.sqrt(sq_b)
    for step in range(ITERS):
        if step > 0:
            _, (step_x, part_y), _ = _rounds("region", [local_x, local_y])
            partial_value = transposed_product(dual)
            grad, (step_y,), _ = _rounds("col", [part_y], split=partial_value)
            weight = jnp.sqrt(weight * jnp.sqrt((step_x + 1e-06) / (step_y + 1e-06)))
        tau = (eta / weight)[None, :, None]
        sigma = (eta * weight)[None, :, None]
        new_primal = jnp.clip(primal_reg - tau * (cost_reg - grad), 0.0, upper_reg)
        point = 2.0 * new_primal - primal_reg
        product = product_of(point)
        new_dual = jnp.maximum(dual + sigma * (rhs[:, None, :] - product), 0.0)
        local_x = jnp.sum((new_primal - primal_reg) ** 2, axis=(0, 2))
        local_y = jnp.sum((new_dual - dual) ** 2, axis=(0, 2))
        primal_reg, dual = (new_primal, new_dual)
    _, (step_x, part_y), _ = _rounds("region", [local_x, local_y])
    _, (step_y,), _ = _rounds("col", [part_y])
    weight = jnp.sqrt(weight * jnp.sqrt((step_x + 1e-06) / (step_y + 1e-06)))
    primal_out = lax.dynamic_slice_in_dim(
        primal_reg, _slot(me, ncol) * own_blocks, own_blocks, axis=0
    )
    return (primal_out, dual, weight)


def solution(mesh):
    placed = (
        P(("region", "col"), None, None),
        P(("region", "col")),
        P(("region", "col")),
        P(("region", "col")),
        P(("region", "col"), None),
        P(("region", "col"), None),
        P(("region", "col"), None),
        P(("region", "col"), None, None),
        P(("region", "col"), None, None),
        P(),
        P(),
    )
    return jax.shard_map(
        local,
        mesh=mesh,
        in_specs=placed,
        out_specs=(P(("region", "col"), None, None), P(("region", "col"), None, None), P()),
        check_vma=False,
    )
```

```python
import jax
import jax.numpy as jnp
from jax import lax
from jax.sharding import PartitionSpec as P

ITERS = 2


def _pow2(n):
    return n >= 1 and (n & (n - 1)) == 0


def _exchange(x, axis, n, bit):
    return lax.ppermute(x, axis, [(i, i ^ (1 << bit)) for i in range(n)])


def _gather_order(n):
    bits = n.bit_length() - 1
    return list(range(1, bits)) + [0] if bits > 1 else list(range(bits))


def _slot(index, n):
    out = 0
    for m, bit in enumerate(_gather_order(n)):
        out = out + (((index >> bit) & 1) << m)
    return out


def _rounds(axis, sums, own=None, split=None):
    n = lax.axis_size(axis)
    if not _pow2(n) or n < 2:
        sums = [lax.psum(s, axis) for s in sums]
        full = None if split is None else lax.psum(split, axis)
        if own is not None:
            own = lax.all_gather(own, axis, axis=0, tiled=False)
        return full, sums, own
    shapes = [s.shape for s in sums]
    sizes = [s.size for s in sums]
    me = lax.axis_index(axis)
    order = _gather_order(n)
    bits = n.bit_length() - 1
    buf = None
    if own is not None:
        assert split is not None
        mine_slot = _slot(me, n)
        buf = jnp.zeros((n,) + own.shape, own.dtype)
        buf = lax.dynamic_update_index_in_dim(buf, own, mine_slot, 0)
    if split is not None:
        half = lax.rem(me, 2)
        halves = split.reshape((2, split.shape[0] // 2) + split.shape[1:])
        keep = lax.dynamic_index_in_dim(halves, half, 0, keepdims=False)
        give = lax.dynamic_index_in_dim(halves, 1 - half, 0, keepdims=False)
    steps = list(range(bits)) + ([0] if split is not None else [])
    m = 0
    for step, bit in enumerate(steps):
        last = split is not None and step == bits
        parts = []
        if split is not None:
            parts.append((give if step == 0 else keep).reshape(-1))
        if not last:
            parts += [s.reshape(-1) for s in sums]
        carry = buf is not None and m < bits and order[m] == bit and (step > 0 or bits == 1)
        if carry:
            used = sum(p.shape[0] for p in parts)
            if used % 1024:
                parts.append(jnp.zeros((-used % 1024,), jnp.float32))
            start = (mine_slot >> m) << m
            parts.append(lax.dynamic_slice_in_dim(buf, start, 1 << m, axis=0).reshape(-1))
        flat = jnp.concatenate(parts) if len(parts) > 1 else parts[0]
        got = _exchange(flat, axis, n, bit)
        off = 0
        if split is not None:
            piece = got[: keep.size].reshape(keep.shape)
            if last:
                other = piece
            else:
                keep = keep + piece
            off = keep.size
        if not last:
            new_sums = []
            for shape, size, s in zip(shapes, sizes, sums):
                new_sums.append(s + got[off : off + size].reshape(shape))
                off += size
            sums = new_sums
        if carry:
            off += -off % 1024
            theirs = ((mine_slot ^ (1 << m)) >> m) << m
            chunk = got[off:].reshape((1 << m,) + own.shape)
            buf = lax.dynamic_update_slice_in_dim(buf, chunk, theirs, axis=0)
            m += 1
    full = None
    if split is not None:
        both = jnp.concatenate([keep, other, keep], axis=0)
        full = lax.dynamic_slice_in_dim(both, half * keep.shape[0], 2 * keep.shape[0], axis=0)
    return full, sums, buf


def local(
    tiles,
    tile_rows,
    tile_cols,
    tile_count,
    rhs,
    base_cost,
    upper,
    primal,
    dual,
    price_levels,
    scenario_ids,
):
    hp = lax.Precision.HIGHEST
    ntiles = tiles.shape[0]
    row_blocks = rhs.shape[0]
    own_blocks = base_cost.shape[0]
    scenarios = primal.shape[1]
    lanes = primal.shape[2]
    ncol = lax.axis_size("col")
    region_blocks = own_blocks * ncol
    devices = lax.axis_size(("region", "col"))
    me = lax.axis_index("col")
    live = (jnp.arange(ntiles, dtype=jnp.int32) < tile_count[0]).astype(jnp.float32)
    choose = (
        scenario_ids[:, None] == jnp.arange(price_levels.shape[0], dtype=jnp.int32)[None, :]
    ).astype(jnp.float32)
    factor = jnp.dot(choose, price_levels, precision=hp)
    cost = base_cost[:, None, :] * factor[None, :, :]
    local_a = jnp.sum(tiles * tiles * live[:, None, None], axis=(0, 1))
    local_c = jnp.sum(cost * cost, axis=(0, 2))
    local_b = jnp.sum(rhs * rhs, axis=0)
    width = scenarios * lanes

    slot_cols = _slot(tile_cols // own_blocks, ncol) * own_blocks + tile_cols % own_blocks
    place = slot_cols * row_blocks + tile_rows
    place_live = (
        place[None, :] == jnp.arange(region_blocks * row_blocks, dtype=jnp.int32)[:, None]
    ).astype(jnp.float32) * live[None, :]
    dense = jnp.dot(place_live, tiles.reshape(ntiles, -1), precision=hp)
    dense = dense.reshape(region_blocks, row_blocks, tiles.shape[1], tiles.shape[2])
    dense = dense.transpose(1, 2, 0, 3)

    def transposed_product(dual):
        return jnp.einsum("rsi,ricj->csj", dual, dense, precision=lax.Precision.HIGH)

    def product_of(point):
        return jnp.einsum("ricj,csj->rsi", dense, point, precision=lax.Precision.HIGH)

    norms = jnp.concatenate([local_a, local_b, local_c])
    n_region = lax.axis_size("region")
    if _pow2(n_region) and n_region >= 2:
        norms = norms + _exchange(norms, "region", n_region, 0)
        norms, dense = lax.optimization_barrier((norms, dense))
        for bit in range(1, n_region.bit_length() - 1):
            norms = norms + _exchange(norms, "region", n_region, bit)
    else:
        norms = lax.psum(norms, "region")
    own_rows = own_blocks * (scenarios + 2)
    own = jnp.concatenate(
        [
            primal.reshape(own_blocks * scenarios, lanes),
            base_cost,
            upper,
            jnp.zeros((-own_rows % 8, lanes), jnp.float32),
        ],
        axis=0,
    )
    partial_value = transposed_product(dual)
    grad, (norms,), gathered = _rounds("col", [norms], own, split=partial_value)
    sq_a = jnp.sum(norms[:lanes])
    sq_b = jnp.sum(norms[lanes : 2 * lanes])
    sq_c = norms[2 * lanes :]
    primal_reg = gathered[:, : own_blocks * scenarios].reshape(region_blocks, scenarios, lanes)
    base_reg = gathered[:, own_blocks * scenarios : own_blocks * (scenarios + 1)]
    upper_reg = gathered[:, own_blocks * (scenarios + 1) : own_rows]
    cost_reg = base_reg.reshape(region_blocks, lanes)[:, None, :] * factor[None, :, :]
    upper_reg = upper_reg.reshape(region_blocks, lanes)[:, None, :]
    eta = 0.5 / jnp.sqrt(sq_a / (lanes * row_blocks * devices))
    weight = jnp.sqrt(sq_c) / jnp.sqrt(sq_b)
    for step in range(ITERS):
        if step > 0:
            _, (step_x, part_y), _ = _rounds("region", [local_x, local_y])
            partial_value = transposed_product(dual)
            grad, (step_y,), _ = _rounds("col", [part_y], split=partial_value)
            weight = jnp.sqrt(weight * jnp.sqrt((step_x + 1e-06) / (step_y + 1e-06)))
        tau = (eta / weight)[None, :, None]
        sigma = (eta * weight)[None, :, None]
        new_primal = jnp.clip(primal_reg - tau * (cost_reg - grad), 0.0, upper_reg)
        point = 2.0 * new_primal - primal_reg
        product = product_of(point)
        new_dual = jnp.maximum(dual + sigma * (rhs[:, None, :] - product), 0.0)
        local_x = jnp.sum((new_primal - primal_reg) ** 2, axis=(0, 2))
        local_y = jnp.sum((new_dual - dual) ** 2, axis=(0, 2))
        primal_reg, dual = (new_primal, new_dual)
    _, (part_y,), _ = _rounds("col", [local_y])
    _, (step_x, step_y), _ = _rounds("region", [local_x, part_y])
    weight = jnp.sqrt(weight * jnp.sqrt((step_x + 1e-06) / (step_y + 1e-06)))
    primal_out = lax.dynamic_slice_in_dim(
        primal_reg, _slot(me, ncol) * own_blocks, own_blocks, axis=0
    )
    return (primal_out, dual, weight)


def solution(mesh):
    placed = (
        P(("region", "col"), None, None),
        P(("region", "col")),
        P(("region", "col")),
        P(("region", "col")),
        P(("region", "col"), None),
        P(("region", "col"), None),
        P(("region", "col"), None),
        P(("region", "col"), None, None),
        P(("region", "col"), None, None),
        P(),
        P(),
    )
    return jax.shard_map(
        local,
        mesh=mesh,
        in_specs=placed,
        out_specs=(P(("region", "col"), None, None), P(("region", "col"), None, None), P()),
        check_vma=False,
    )
```
